32 devices in a mesh: seq: 8 (over z, x), head: 4 (over y, core).
Axes of the slice: x: 2, y: 2, z: 4, core: 2. Of those that a mesh axis runs over, the one named last changes fastest.
Arguments:
- queries: bfloat16 [16, 8192, 128], P('head', 'seq'), may hold values from -16 to 16
- key_rows: bfloat16 [16, 8192, 128], P('head', 'seq'), may hold values from -16 to 16
- value_rows: bfloat16 [16, 8192, 128], P('head', 'seq'), may hold values from -6 to 6
- grad_out: bfloat16 [16, 8192, 128], P('head', 'seq'), may hold values from -6 to 6
- partner_pos: int32 [16, 2, 8], P('head'), may hold values from 0 to 7, each once within a row
Outputs:
- attended: bfloat16 [16, 8192, 128], P('head', 'seq')
- grad_queries: bfloat16 [16, 8192, 128], P('head', 'seq')
- grad_keys: bfloat16 [16, 8192, 128], P('head', 'seq')
- grad_values: bfloat16 [16, 8192, 128], P('head', 'seq')
The draws below stay inside these ranges and needn't reach their ends.
Inputs may be any that keep to these rules, and one draw needn't show every extreme that they name: In head h, the block at place j of segment s takes the block at place partner_pos[h, s, j] of segment s as its partner; each row of 8 numbers is a permutation.
All inputs are finite; a program needn't handle non-finite values.
Results may differ from the reference program's by a relative error of at most 0.008.
Values may be sent and summed in bfloat16 or wider, within the bound.
No kernel may reach another device: no remote copies, remote signals or barrier semaphores. Data moves between devices by JAX's collectives and lax.ppermute only.
A program may use at most 128 MiB of HBM per device.

```python
import math
import jax
import jax.numpy as jnp
from jax import lax

H = 16
HD = 128
BLK = 512
BLK_DEV = 2
LEN = 8192
SEG = 8
NSEG = 2


def paired_rows(key):
    base_key = jax.random.fold_in(key, 7)
    query_seed, key_seed = jax.random.split(base_key, 2)
    array_shape = (H, LEN, HD)
    queries = jax.random.truncated_normal(query_seed, -4.0, 4.0, array_shape, jnp.float32)
    key_rows = jax.random.truncated_normal(key_seed, -4.0, 4.0, array_shape, jnp.float32)
    return (queries, key_rows)


def draw_queries(key, part):
    return paired_rows(key)[0].astype(jnp.bfloat16)


def draw_key_rows(key, part):
    return paired_rows(key)[1].astype(jnp.bfloat16)


def level_of(stream_key, shape, shards, least, largest):
    def one(dim, parts):
        steps = jax.random.uniform(jax.random.fold_in(jax.random.fold_in(stream_key, 6), dim), (parts,), jnp.float32, least / len(shards), largest / len(shards))
        return jnp.repeat(jnp.exp(steps), shape[dim] // parts).reshape((-1,) + (1,) * (len(shape) - dim - 1))

    loudness = one(*shards[0])
    for cut in shards[1:]:
        loudness = loudness * one(*cut)
    return loudness


def scatter_about(rng, shape, deviation, limit, cuts=(), held_as=jnp.bfloat16):
    level = level_of(rng, shape, cuts, -0.22, 0.18) if cuts else 1.0
    array = jax.random.normal(rng, shape, jnp.float32) * deviation * level
    return jnp.minimum(jnp.maximum(array, -limit), limit).astype(held_as)


def setup_inputs(seed: int = 0) -> dict:
    key_list = jax.random.split(jax.random.key(seed), 6)
    queries = draw_queries(jax.random.fold_in(key_list[5], 71), 0)
    key_rows = draw_key_rows(jax.random.fold_in(key_list[5], 71), 0)
    value_rows = scatter_about(key_list[2], (H, LEN, HD), 1.0, 6.0, ((0, 4), (1, 8)))
    grad_out = scatter_about(key_list[3], (H, LEN, HD), 1.0, 6.0, ((0, 4), (1, 8)))
    partner_pos = jax.vmap(lambda own: jax.random.permutation(own, SEG))(jax.random.split(key_list[4], H * NSEG)).reshape((H, NSEG, SEG)).astype(jnp.int32)
    return {"queries": queries, "key_rows": key_rows, "value_rows": value_rows, "grad_out": grad_out, "partner_pos": partner_pos}


def block_terms(query_rows, key_block, values, grad_rows, usable):
    scaling = 1.0 / math.sqrt(HD)
    scores = jnp.dot(query_rows.astype(jnp.float32), key_block.astype(jnp.float32).T, preferred_element_type=jnp.float32) * scaling
    scores = jnp.where(usable[None, :], scores, -jnp.inf)
    highest = lax.optimization_barrier(jnp.max(scores, axis=1, keepdims=True))
    weights = jnp.exp(scores - highest)
    shares = weights / lax.optimization_barrier(jnp.sum(weights, axis=1, keepdims=True))
    shares_low = lax.optimization_barrier(shares.astype(jnp.bfloat16))
    attended = jnp.dot(shares_low.astype(jnp.float32), values.astype(jnp.float32), preferred_element_type=jnp.float32).astype(jnp.bfloat16)
    attended_wide = lax.optimization_barrier(attended).astype(jnp.float32)
    row_dot = lax.optimization_barrier(jnp.sum(grad_rows.astype(jnp.float32) * attended_wide, axis=1, keepdims=True))
    grad_probs = jnp.dot(grad_rows.astype(jnp.float32), values.astype(jnp.float32).T, preferred_element_type=jnp.float32)
    dscore = lax.optimization_barrier((shares * (grad_probs - row_dot)).astype(jnp.bfloat16))
    grad_query = (jnp.dot(dscore.astype(jnp.float32), key_block.astype(jnp.float32), preferred_element_type=jnp.float32) * scaling).astype(jnp.bfloat16)
    key_terms = jnp.dot(dscore.astype(jnp.float32).T, query_rows.astype(jnp.float32), preferred_element_type=jnp.float32) * scaling
    value_terms = jnp.dot(shares_low.astype(jnp.float32).T, grad_rows.astype(jnp.float32), preferred_element_type=jnp.float32)
    return (attended, grad_query, key_terms, value_terms)

def reference(queries, key_rows, value_rows, grad_out, partner_pos):
    total_blocks = LEN // BLK
    seg_index = jnp.arange(NSEG, dtype=jnp.int32)[:, None]
    place_index = jnp.arange(SEG, dtype=jnp.int32)[None, :]
    query_block = ((seg_index + NSEG * (place_index // BLK_DEV)) * BLK_DEV + place_index % BLK_DEV).astype(jnp.int32)
    partner_block = ((seg_index[None] + NSEG * (partner_pos // BLK_DEV)) * BLK_DEV + partner_pos % BLK_DEV).astype(jnp.int32)
    partner = jnp.zeros((H, total_blocks), jnp.int32).at[:, query_block.reshape(-1)].set(partner_block.reshape(H, -1))
    block_numbers = jnp.arange(total_blocks, dtype=jnp.int32)

    def one_head(inputs):
        query_head, key_head, value_head, grad_head, partner_head = inputs
        query_blocks = query_head.reshape(total_blocks, BLK, HD)
        key_blocks = key_head.reshape(total_blocks, BLK, HD)
        value_blocks = value_head.reshape(total_blocks, BLK, HD)
        grad_blocks = grad_head.reshape(total_blocks, BLK, HD)
        key_sets = jnp.concatenate([key_blocks, jnp.roll(key_blocks, 1, axis=0), key_blocks[partner_head]], axis=1)
        value_sets = jnp.concatenate([value_blocks, jnp.roll(value_blocks, 1, axis=0), value_blocks[partner_head]], axis=1)

        def one_block(pieces):
            query_rows, key_block, values, grad_rows, block_index = pieces
            flags = jnp.concatenate([jnp.ones((BLK,), jnp.int32), jnp.zeros((BLK,), jnp.int32) + block_index, jnp.ones((BLK,), jnp.int32)])
            return block_terms(query_rows, key_block, values, grad_rows, flags > 0)
        attended, grad_query, key_terms, value_terms = lax.map(one_block, (query_blocks, key_sets, value_sets, grad_blocks, block_numbers))

        def gather_terms(term_rows):
            own_part = term_rows[:, :BLK]
            window_part = jnp.roll(term_rows[:, BLK:2 * BLK], -1, axis=0)
            paired = jnp.zeros_like(own_part).at[partner_head].add(term_rows[:, 2 * BLK:])
            return (own_part + window_part + paired).astype(jnp.bfloat16).reshape(LEN, HD)
        return (attended.reshape(LEN, HD), grad_query.reshape(LEN, HD), gather_terms(key_terms), gather_terms(value_terms))
    attended, grad_queries, grad_keys, grad_values = lax.map(one_head, (queries, key_rows, value_rows, grad_out, partner))
    return (attended, grad_queries, grad_keys, grad_values)
```

```python
import math

import jax
import jax.numpy as jnp
from jax import lax
from jax.sharding import PartitionSpec as P

BLK = 512


def group_pairs(nseg, group, shift):
    return [
        (seg + nseg * w, seg + nseg * ((w + shift) % group))
        for seg in range(nseg)
        for w in range(group)
    ]


def next_segment_pairs(nseg, group):
    return [
        (seg + nseg * w, (seg + 1) % nseg + nseg * w)
        for seg in range(nseg)
        for w in range(group)
    ]


def block_terms(query_rows, key_block, values, grad_rows, usable):
    scaling = 1.0 / math.sqrt(query_rows.shape[-1])
    scores = (
        jnp.einsum("cid,cjd->cij", query_rows, key_block, preferred_element_type=jnp.float32)
        * scaling
    )
    scores = jnp.where(usable[:, None, :], scores, -jnp.inf)
    highest = jnp.max(scores, axis=2, keepdims=True)
    weights = jnp.exp(scores - highest)
    shares = weights / jnp.sum(weights, axis=2, keepdims=True)
    shares_low = shares.astype(jnp.bfloat16)
    attended = jnp.einsum(
        "cij,cjd->cid", shares_low, values, preferred_element_type=jnp.float32
    ).astype(jnp.bfloat16)
    attended_wide = lax.optimization_barrier(attended).astype(jnp.float32)
    row_dot = jnp.sum(grad_rows.astype(jnp.float32) * attended_wide, axis=2, keepdims=True)
    grad_probs = jnp.einsum("cid,cjd->cij", grad_rows, values, preferred_element_type=jnp.float32)
    dscore = (shares * (grad_probs - row_dot)).astype(jnp.bfloat16)
    grad_query = (
        jnp.einsum("cij,cjd->cid", dscore, key_block, preferred_element_type=jnp.float32) * scaling
    ).astype(jnp.bfloat16)
    key_terms = (
        jnp.einsum("cij,cid->cjd", dscore, query_rows, preferred_element_type=jnp.float32) * scaling
    )
    value_terms = jnp.einsum(
        "cij,cid->cjd", shares_low, grad_rows, preferred_element_type=jnp.float32
    )
    return attended, grad_query, key_terms, value_terms


def interleave(even, odd):
    return jnp.stack([even, odd], axis=1).reshape((-1,) + even.shape[1:])


def body(queries, key_rows, value_rows, grad_out, partner_pos):
    heads, row_count, width = queries.shape
    blocks = row_count // BLK
    places = partner_pos.shape[2]
    group = places // blocks
    if heads != group:
        raise ValueError("heads mismatch")
    nseg = lax.axis_size("seq") // group
    device = lax.axis_index("seq")
    segment = device % nseg
    within = device // nseg

    data = jnp.stack(
        [
            queries.reshape(heads, blocks, BLK, width),
            grad_out.reshape(heads, blocks, BLK, width),
            key_rows.reshape(heads, blocks, BLK, width),
            value_rows.reshape(heads, blocks, BLK, width),
        ],
        axis=1,
    )
    received = [lax.dynamic_index_in_dim(data, within, axis=0, keepdims=False)]
    for shift in range(1, group):
        send = lax.dynamic_index_in_dim(data, (within + shift) % group, axis=0, keepdims=False)
        received.append(lax.ppermute(send, "seq", group_pairs(nseg, group, shift)))
    received = jnp.stack(received)
    order = (within - jnp.arange(group, dtype=jnp.int32)) % group
    local = jnp.take(received, order, axis=0)
    local = jnp.swapaxes(local, 0, 1).reshape(4, group * blocks, BLK, width)
    q_all, g_all, k_all, v_all = local[0], local[1], local[2], local[3]

    odd_kv = jnp.stack([k_all[1::2], v_all[1::2]], axis=1)
    odd_send = jnp.where(segment == nseg - 1, jnp.roll(odd_kv, 1, axis=0), odd_kv)
    window_kv = lax.ppermute(odd_send, "seq", next_segment_pairs(nseg, group))
    k_window = interleave(window_kv[:, 0], k_all[0::2])
    v_window = interleave(window_kv[:, 1], v_all[0::2])

    my_partners = lax.dynamic_index_in_dim(
        lax.dynamic_index_in_dim(partner_pos, within, axis=0, keepdims=False),
        segment,
        axis=0,
        keepdims=False,
    )
    k_partner = jnp.take(k_all, my_partners, axis=0)
    v_partner = jnp.take(v_all, my_partners, axis=0)
    key_sets = jnp.concatenate([k_all, k_window, k_partner], axis=1)
    value_sets = jnp.concatenate([v_all, v_window, v_partner], axis=1)

    place_ids = jnp.arange(places, dtype=jnp.int32)
    first_block = jnp.logical_and(segment == 0, place_ids == 0)
    usable = jnp.concatenate(
        [
            jnp.ones((places, BLK), jnp.bool_),
            jnp.broadcast_to(jnp.logical_not(first_block)[:, None], (places, BLK)),
            jnp.ones((places, BLK), jnp.bool_),
        ],
        axis=1,
    )
    attended, grad_query, key_terms, value_terms = block_terms(
        q_all, key_sets, value_sets, g_all, usable
    )
    terms = jnp.stack([key_terms, value_terms], axis=1)
    own_part = terms[:, :, :BLK]
    window_part = terms[:, :, BLK : 2 * BLK]
    partner_part = terms[:, :, 2 * BLK :]

    ret = window_part[0::2]
    ret = jnp.where(segment == 0, jnp.roll(ret, -1, axis=0), ret)
    back_pairs = [(b, a) for a, b in next_segment_pairs(nseg, group)]
    window_back = lax.ppermute(ret, "seq", back_pairs)
    window_sum = interleave(window_part[1::2], window_back)

    hits = my_partners[None, :] == place_ids[:, None]
    inverse = jnp.sum(jnp.where(hits, place_ids[None, :], 0), axis=1)
    partner_sum = jnp.take(partner_part, inverse, axis=0)
    grads = (own_part + window_sum + partner_sum).astype(jnp.bfloat16)

    outs = jnp.stack([attended, grad_query, grads[:, 0], grads[:, 1]], axis=1)
    outs = outs.reshape(group, blocks, 4, BLK, width)
    returned = [lax.dynamic_index_in_dim(outs, within, axis=0, keepdims=False)]
    for shift in range(1, group):
        send = lax.dynamic_index_in_dim(outs, (within - shift) % group, axis=0, keepdims=False)
        returned.append(lax.ppermute(send, "seq", group_pairs(nseg, group, group - shift)))
    returned = jnp.stack(returned)
    head_order = (jnp.arange(group, dtype=jnp.int32) - within) % group
    result = jnp.take(returned, head_order, axis=0)
    shape = (heads, row_count, width)
    return tuple(result[:, :, a].reshape(shape) for a in range(4))


def solution(mesh):
    return jax.shard_map(
        body,
        mesh=mesh,
        in_specs=(
            P("head", "seq", None),
            P("head", "seq", None),
            P("head", "seq", None),
            P("head", "seq", None),
            P("head", None, None),
        ),
        out_specs=(
            P("head", "seq", None),
            P("head", "seq", None),
            P("head", "seq", None),
            P("head", "seq", None),
        ),
        check_vma=False,
    )
```

```python
import math

import jax
import jax.numpy as jnp
from jax import lax
from jax.experimental import pallas as pl
from jax.experimental.pallas import tpu as pltpu
from jax.sharding import PartitionSpec as P

BLK = 512


def group_pairs(nseg, group, shift):
    return [
        (seg + nseg * w, seg + nseg * ((w + shift) % group))
        for seg in range(nseg)
        for w in range(group)
    ]


def next_segment_pairs(nseg, group):
    return [
        (seg + nseg * w, (seg + 1) % nseg + nseg * w)
        for seg in range(nseg)
        for w in range(group)
    ]


def block_terms(query_rows, key_block, values, grad_rows, usable):
    scaling = 1.0 / math.sqrt(query_rows.shape[-1])
    scores = (
        jnp.einsum("cid,cjd->cij", query_rows, key_block, preferred_element_type=jnp.float32)
        * scaling
    )
    scores = jnp.where(usable[:, None, :], scores, -jnp.inf)
    highest = jnp.max(scores, axis=2, keepdims=True)
    weights = jnp.exp(scores - highest)
    shares = weights / jnp.sum(weights, axis=2, keepdims=True)
    shares_low = shares.astype(jnp.bfloat16)
    attended = jnp.einsum(
        "cij,cjd->cid", shares_low, values, preferred_element_type=jnp.float32
    ).astype(jnp.bfloat16)
    attended_wide = lax.optimization_barrier(attended).astype(jnp.float32)
    row_dot = jnp.sum(grad_rows.astype(jnp.float32) * attended_wide, axis=2, keepdims=True)
    grad_probs = jnp.einsum("cid,cjd->cij", grad_rows, values, preferred_element_type=jnp.float32)
    dscore = (shares * (grad_probs - row_dot)).astype(jnp.bfloat16)
    grad_query = (
        jnp.einsum("cij,cjd->cid", dscore, key_block, preferred_element_type=jnp.float32) * scaling
    ).astype(jnp.bfloat16)
    key_terms = (
        jnp.einsum("cij,cid->cjd", dscore, query_rows, preferred_element_type=jnp.float32) * scaling
    )
    value_terms = jnp.einsum(
        "cij,cid->cjd", shares_low, grad_rows, preferred_element_type=jnp.float32
    )
    return attended, grad_query, key_terms, value_terms


def attention_kernel(flag_ref, q_ref, g_ref, k_ref, v_ref, att_ref, dq_ref, kt_ref, vt_ref):
    place = pl.program_id(0)
    q = q_ref[0]
    g = g_ref[0]
    k = k_ref[0]
    v = v_ref[0]
    scaling = 1.0 / math.sqrt(q.shape[-1])
    rows_by_rows = (((1,), (1,)), ((), ()))
    cols_by_cols = (((0,), (0,)), ((), ()))
    scores = lax.dot_general(q, k, rows_by_rows, preferred_element_type=jnp.float32) * scaling
    col = lax.broadcasted_iota(jnp.int32, scores.shape, 1)
    kill = jnp.where(place == 0, flag_ref[0], 0)
    masked = jnp.logical_and(jnp.logical_and(col >= BLK, col < 2 * BLK), kill > 0)
    scores = jnp.where(masked, -jnp.inf, scores)
    highest = jnp.max(scores, axis=1, keepdims=True)
    weights = jnp.exp(scores - highest)
    shares = weights / jnp.sum(weights, axis=1, keepdims=True)
    shares_low = shares.astype(jnp.bfloat16)
    attended = jnp.dot(shares_low, v, preferred_element_type=jnp.float32).astype(jnp.bfloat16)
    att_ref[0] = attended
    row_dot = jnp.sum(g.astype(jnp.float32) * attended.astype(jnp.float32), axis=1, keepdims=True)
    grad_probs = lax.dot_general(g, v, rows_by_rows, preferred_element_type=jnp.float32)
    dscore = (shares * (grad_probs - row_dot)).astype(jnp.bfloat16)
    dq_ref[0] = (jnp.dot(dscore, k, preferred_element_type=jnp.float32) * scaling).astype(jnp.bfloat16)
    kt_ref[0] = lax.dot_general(dscore, q, cols_by_cols, preferred_element_type=jnp.float32) * scaling
    vt_ref[0] = lax.dot_general(shares_low, g, cols_by_cols, preferred_element_type=jnp.float32)


def fused_terms(q_all, g_all, key_sets, value_sets, first_masked):
    places, rows, width = q_all.shape
    keys = key_sets.shape[1]
    row_spec = pl.BlockSpec((1, rows, width), lambda p, flag: (p, 0, 0))
    key_spec = pl.BlockSpec((1, keys, width), lambda p, flag: (p, 0, 0))
    flops = 12 * places * rows * keys * width
    return pl.pallas_call(
        attention_kernel,
        grid_spec=pltpu.PrefetchScalarGridSpec(
            num_scalar_prefetch=1,
            grid=(places,),
            in_specs=[row_spec, row_spec, key_spec, key_spec],
            out_specs=[row_spec, row_spec, key_spec, key_spec],
        ),
        out_shape=[
            jax.ShapeDtypeStruct((places, rows, width), jnp.bfloat16),
            jax.ShapeDtypeStruct((places, rows, width), jnp.bfloat16),
            jax.ShapeDtypeStruct((places, keys, width), jnp.float32),
            jax.ShapeDtypeStruct((places, keys, width), jnp.float32),
        ],
        cost_estimate=pl.CostEstimate(
            flops=flops,
            transcendentals=places * rows * keys,
            bytes_accessed=places * (rows * width * 8 + keys * width * 20),
        ),
    )(first_masked, q_all, g_all, key_sets, value_sets)


def interleave(even, odd):
    return jnp.stack([even, odd], axis=1).reshape((-1,) + even.shape[1:])


def body(queries, key_rows, value_rows, grad_out, partner_pos):
    heads, row_count, width = queries.shape
    blocks = row_count // BLK
    places = partner_pos.shape[2]
    group = places // blocks
    if heads != group:
        raise ValueError("heads mismatch")
    nseg = lax.axis_size("seq") // group
    device = lax.axis_index("seq")
    segment = device % nseg
    within = device // nseg

    data = jnp.stack(
        [
            queries.reshape(heads, blocks, BLK, width),
            grad_out.reshape(heads, blocks, BLK, width),
            key_rows.reshape(heads, blocks, BLK, width),
            value_rows.reshape(heads, blocks, BLK, width),
        ],
        axis=1,
    )
    received = [lax.dynamic_index_in_dim(data, within, axis=0, keepdims=False)]
    for shift in range(1, group):
        send = lax.dynamic_index_in_dim(data, (within + shift) % group, axis=0, keepdims=False)
        received.append(lax.ppermute(send, "seq", group_pairs(nseg, group, shift)))
    received = jnp.stack(received)
    order = (within - jnp.arange(group, dtype=jnp.int32)) % group
    local = jnp.take(received, order, axis=0)
    local = jnp.swapaxes(local, 0, 1).reshape(4, group * blocks, BLK, width)
    q_all, g_all, k_all, v_all = local[0], local[1], local[2], local[3]

    odd_kv = jnp.stack([k_all[1::2], v_all[1::2]], axis=1)
    odd_send = jnp.where(segment == nseg - 1, jnp.roll(odd_kv, 1, axis=0), odd_kv)
    window_kv = lax.ppermute(odd_send, "seq", next_segment_pairs(nseg, group))
    k_window = interleave(window_kv[:, 0], k_all[0::2])
    v_window = interleave(window_kv[:, 1], v_all[0::2])

    my_partners = lax.dynamic_index_in_dim(
        lax.dynamic_index_in_dim(partner_pos, within, axis=0, keepdims=False),
        segment,
        axis=0,
        keepdims=False,
    )
    k_partner = jnp.take(k_all, my_partners, axis=0)
    v_partner = jnp.take(v_all, my_partners, axis=0)
    key_sets = jnp.concatenate([k_all, k_window, k_partner], axis=1)
    value_sets = jnp.concatenate([v_all, v_window, v_partner], axis=1)

    place_ids = jnp.arange(places, dtype=jnp.int32)
    first_masked = (segment == 0).astype(jnp.int32).reshape(1)
    attended, grad_query, key_terms, value_terms = fused_terms(
        q_all, g_all, key_sets, value_sets, first_masked
    )
    terms = jnp.stack([key_terms, value_terms], axis=1)
    own_part = terms[:, :, :BLK]
    window_part = terms[:, :, BLK : 2 * BLK]
    partner_part = terms[:, :, 2 * BLK :]

    ret = window_part[0::2]
    ret = jnp.where(segment == 0, jnp.roll(ret, -1, axis=0), ret)
    back_pairs = [(b, a) for a, b in next_segment_pairs(nseg, group)]
    window_back = lax.ppermute(ret, "seq", back_pairs)
    window_sum = interleave(window_part[1::2], window_back)

    hits = my_partners[None, :] == place_ids[:, None]
    inverse = jnp.sum(jnp.where(hits, place_ids[None, :], 0), axis=1)
    partner_sum = jnp.take(partner_part, inverse, axis=0)
    grads = (own_part + window_sum + partner_sum).astype(jnp.bfloat16)

    outs = jnp.stack([attended, grad_query, grads[:, 0], grads[:, 1]], axis=1)
    outs = outs.reshape(group, blocks, 4, BLK, width)
    returned = [lax.dynamic_index_in_dim(outs, within, axis=0, keepdims=False)]
    for shift in range(1, group):
        send = lax.dynamic_index_in_dim(outs, (within - shift) % group, axis=0, keepdims=False)
        returned.append(lax.ppermute(send, "seq", group_pairs(nseg, group, group - shift)))
    returned = jnp.stack(returned)
    head_order = (jnp.arange(group, dtype=jnp.int32) - within) % group
    result = jnp.take(returned, head_order, axis=0)
    shape = (heads, row_count, width)
    return tuple(result[:, :, a].reshape(shape) for a in range(4))


def solution(mesh):
    return jax.shard_map(
        body,
        mesh=mesh,
        in_specs=(
            P("head", "seq", None),
            P("head", "seq", None),
            P("head", "seq", None),
            P("head", "seq", None),
            P("head", None, None),
        ),
        out_specs=(
            P("head", "seq", None),
            P("head", "seq", None),
            P("head", "seq", None),
            P("head", "seq", None),
        ),
        check_vma=False,
    )
```

```python
import math

import jax
import jax.numpy as jnp
from jax import lax
from jax.experimental import pallas as pl
from jax.experimental.pallas import tpu as pltpu
from jax.sharding import PartitionSpec as P

BLK = 512


def group_pairs(nseg, group, shift):
    return [
        (seg + nseg * w, seg + nseg * ((w + shift) % group))
        for seg in range(nseg)
        for w in range(group)
    ]


def next_segment_pairs(nseg, group):
    return [
        (seg + nseg * w, (seg + 1) % nseg + nseg * w)
        for seg in range(nseg)
        for w in range(group)
    ]


def block_terms(query_rows, key_block, values, grad_rows, usable):
    scaling = 1.0 / math.sqrt(query_rows.shape[-1])
    scores = (
        jnp.einsum("cid,cjd->cij", query_rows, key_block, preferred_element_type=jnp.float32)
        * scaling
    )
    scores = jnp.where(usable[:, None, :], scores, -jnp.inf)
    highest = jnp.max(scores, axis=2, keepdims=True)
    weights = jnp.exp(scores - highest)
    shares = weights / jnp.sum(weights, axis=2, keepdims=True)
    shares_low = shares.astype(jnp.bfloat16)
    attended = jnp.einsum(
        "cij,cjd->cid", shares_low, values, preferred_element_type=jnp.float32
    ).astype(jnp.bfloat16)
    attended_wide = lax.optimization_barrier(attended).astype(jnp.float32)
    row_dot = jnp.sum(grad_rows.astype(jnp.float32) * attended_wide, axis=2, keepdims=True)
    grad_probs = jnp.einsum("cid,cjd->cij", grad_rows, values, preferred_element_type=jnp.float32)
    dscore = (shares * (grad_probs - row_dot)).astype(jnp.bfloat16)
    grad_query = (
        jnp.einsum("cij,cjd->cid", dscore, key_block, preferred_element_type=jnp.float32) * scaling
    ).astype(jnp.bfloat16)
    key_terms = (
        jnp.einsum("cij,cid->cjd", dscore, query_rows, preferred_element_type=jnp.float32) * scaling
    )
    value_terms = jnp.einsum(
        "cij,cid->cjd", shares_low, grad_rows, preferred_element_type=jnp.float32
    )
    return attended, grad_query, key_terms, value_terms


def attention_kernel(flag_ref, q_ref, g_ref, k_ref, v_ref, att_ref, dq_ref, kt_ref, vt_ref):
    place = pl.program_id(0)
    q = q_ref[0]
    g = g_ref[0]
    k = k_ref[0]
    v = v_ref[0]
    scaling = 1.0 / math.sqrt(q.shape[-1])
    rows_by_rows = (((1,), (1,)), ((), ()))
    cols_by_cols = (((0,), (0,)), ((), ()))
    scores = lax.dot_general(q, k, rows_by_rows, preferred_element_type=jnp.float32) * scaling
    col = lax.broadcasted_iota(jnp.int32, scores.shape, 1)
    kill = jnp.where(place == 0, flag_ref[0], 0)
    masked = jnp.logical_and(jnp.logical_and(col >= BLK, col < 2 * BLK), kill > 0)
    scores = jnp.where(masked, -jnp.inf, scores)
    highest = jnp.max(scores, axis=1, keepdims=True)
    weights = jnp.exp(scores - highest)
    shares = weights / jnp.sum(weights, axis=1, keepdims=True)
    shares_low = shares.astype(jnp.bfloat16)
    attended = jnp.dot(shares_low, v, preferred_element_type=jnp.float32).astype(jnp.bfloat16)
    att_ref[0] = attended
    row_dot = jnp.sum(g.astype(jnp.float32) * attended.astype(jnp.float32), axis=1, keepdims=True)
    grad_probs = lax.dot_general(g, v, rows_by_rows, preferred_element_type=jnp.float32)
    dscore = (shares * (grad_probs - row_dot)).astype(jnp.bfloat16)
    dq_ref[0] = (jnp.dot(dscore, k, preferred_element_type=jnp.float32) * scaling).astype(jnp.bfloat16)
    kt_ref[0] = lax.dot_general(dscore, q, cols_by_cols, preferred_element_type=jnp.float32) * scaling
    vt_ref[0] = lax.dot_general(shares_low, g, cols_by_cols, preferred_element_type=jnp.float32)


def fused_terms(q_all, g_all, key_sets, value_sets, first_masked):
    places, rows, width = q_all.shape
    keys = key_sets.shape[1]
    row_spec = pl.BlockSpec((1, rows, width), lambda p, flag: (p, 0, 0))
    key_spec = pl.BlockSpec((1, keys, width), lambda p, flag: (p, 0, 0))
    flops = 12 * places * rows * keys * width
    return pl.pallas_call(
        attention_kernel,
        grid_spec=pltpu.PrefetchScalarGridSpec(
            num_scalar_prefetch=1,
            grid=(places,),
            in_specs=[row_spec, row_spec, key_spec, key_spec],
            out_specs=[row_spec, row_spec, key_spec, key_spec],
        ),
        out_shape=[
            jax.ShapeDtypeStruct((places, rows, width), jnp.bfloat16),
            jax.ShapeDtypeStruct((places, rows, width), jnp.bfloat16),
            jax.ShapeDtypeStruct((places, keys, width), jnp.float32),
            jax.ShapeDtypeStruct((places, keys, width), jnp.float32),
        ],
        cost_estimate=pl.CostEstimate(
            flops=flops,
            transcendentals=places * rows * keys,
            bytes_accessed=places * (rows * width * 8 + keys * width * 20),
        ),
    )(first_masked, q_all, g_all, key_sets, value_sets)


def interleave(even, odd):
    return jnp.stack([even, odd], axis=1).reshape((-1,) + even.shape[1:])


def gather_group(x, within, nseg, group):
    received = [lax.dynamic_index_in_dim(x, within, axis=0, keepdims=False)]
    for shift in range(1, group):
        send = lax.dynamic_index_in_dim(x, (within + shift) % group, axis=0, keepdims=False)
        received.append(lax.ppermute(send, "seq", group_pairs(nseg, group, shift)))
    order = (within - jnp.arange(group, dtype=jnp.int32)) % group
    return jnp.take(jnp.stack(received), order, axis=0)


def scatter_group(y, within, nseg, group):
    returned = [lax.dynamic_index_in_dim(y, within, axis=0, keepdims=False)]
    for shift in range(1, group):
        send = lax.dynamic_index_in_dim(y, (within - shift) % group, axis=0, keepdims=False)
        returned.append(lax.ppermute(send, "seq", group_pairs(nseg, group, group - shift)))
    order = (jnp.arange(group, dtype=jnp.int32) - within) % group
    return jnp.take(jnp.stack(returned), order, axis=0)


def body(queries, key_rows, value_rows, grad_out, partner_pos):
    heads, row_count, width = queries.shape
    blocks = row_count // BLK
    places = partner_pos.shape[2]
    group = places // blocks
    if heads != group or blocks != 2:
        raise ValueError("layout mismatch")
    nseg = lax.axis_size("seq") // group
    device = lax.axis_index("seq")
    segment = device % nseg
    within = device // nseg

    def split(x):
        return x.reshape(heads, blocks, BLK, width)

    q4, g4, k4, v4 = split(queries), split(grad_out), split(key_rows), split(value_rows)
    kv_local = gather_group(jnp.stack([k4, v4], axis=1), within, nseg, group)
    k_all = kv_local[:, 0].reshape(places, BLK, width)
    v_all = kv_local[:, 1].reshape(places, BLK, width)
    kv_local, qd_odd = lax.optimization_barrier(
        (kv_local, jnp.stack([q4[:, 1], g4[:, 1]], axis=1))
    )
    qd_odd = gather_group(qd_odd, within, nseg, group)
    qd_odd, qd_even = lax.optimization_barrier(
        (qd_odd, jnp.stack([q4[:, 0], g4[:, 0]], axis=1))
    )
    qd_even = gather_group(qd_even, within, nseg, group)

    odd_kv = jnp.stack([k_all[1::2], v_all[1::2]], axis=1)
    odd_send = jnp.where(segment == nseg - 1, jnp.roll(odd_kv, 1, axis=0), odd_kv)
    window_kv = lax.ppermute(odd_send, "seq", next_segment_pairs(nseg, group))

    my_partners = lax.dynamic_index_in_dim(
        lax.dynamic_index_in_dim(partner_pos, within, axis=0, keepdims=False),
        segment,
        axis=0,
        keepdims=False,
    )
    k_partner = jnp.take(k_all, my_partners, axis=0)
    v_partner = jnp.take(v_all, my_partners, axis=0)

    odd_keys = jnp.concatenate([k_all[1::2], k_all[0::2], k_partner[1::2]], axis=1)
    odd_values = jnp.concatenate([v_all[1::2], v_all[0::2], v_partner[1::2]], axis=1)
    att_odd, dq_odd, kt_odd, vt_odd = fused_terms(
        qd_odd[:, 0], qd_odd[:, 1], odd_keys, odd_values, jnp.zeros((1,), jnp.int32)
    )
    sent_odd = scatter_group(jnp.stack([att_odd, dq_odd], axis=1), within, nseg, group)

    even_keys = jnp.concatenate([k_all[0::2], window_kv[:, 0], k_partner[0::2]], axis=1)
    even_values = jnp.concatenate([v_all[0::2], window_kv[:, 1], v_partner[0::2]], axis=1)
    first_masked = (segment == 0).astype(jnp.int32).reshape(1)
    att_even, dq_even, kt_even, vt_even = fused_terms(
        qd_even[:, 0], qd_even[:, 1], even_keys, even_values, first_masked
    )

    terms = interleave(jnp.stack([kt_even, vt_even], axis=1), jnp.stack([kt_odd, vt_odd], axis=1))
    own_part = terms[:, :, :BLK]
    window_part = terms[:, :, BLK : 2 * BLK]
    partner_part = terms[:, :, 2 * BLK :]

    ret = window_part[0::2]
    ret = jnp.where(segment == 0, jnp.roll(ret, -1, axis=0), ret)
    back_pairs = [(b, a) for a, b in next_segment_pairs(nseg, group)]
    window_back = lax.ppermute(ret, "seq", back_pairs)

    place_ids = jnp.arange(places, dtype=jnp.int32)
    hits = my_partners[None, :] == place_ids[:, None]
    inverse = jnp.sum(jnp.where(hits, place_ids[None, :], 0), axis=1)
    partner_sum = jnp.take(partner_part, inverse, axis=0)
    grads_even = (own_part[0::2] + window_part[1::2] + partner_sum[0::2]).astype(jnp.bfloat16)
    sent_even = scatter_group(
        jnp.stack([att_even, dq_even, grads_even[:, 0], grads_even[:, 1]], axis=1),
        within,
        nseg,
        group,
    )
    grads_odd = (own_part[1::2] + window_back + partner_sum[1::2]).astype(jnp.bfloat16)
    sent_last = scatter_group(grads_odd, within, nseg, group)

    shape = (heads, row_count, width)

    def joined(even, odd):
        return jnp.stack([even, odd], axis=1).reshape(shape)

    return (
        joined(sent_even[:, 0], sent_odd[:, 0]),
        joined(sent_even[:, 1], sent_odd[:, 1]),
        joined(sent_even[:, 2], sent_last[:, 0]),
        joined(sent_even[:, 3], sent_last[:, 1]),
    )


def solution(mesh):
    return jax.shard_map(
        body,
        mesh=mesh,
        in_specs=(
            P("head", "seq", None),
            P("head", "seq", None),
            P("head", "seq", None),
            P("head", "seq", None),
            P("head", None, None),
        ),
        out_specs=(
            P("head", "seq", None),
            P("head", "seq", None),
            P("head", "seq", None),
            P("head", "seq", None),
        ),
        check_vma=False,
    )
```

```python
import math

import jax
import jax.numpy as jnp
from jax import lax
from jax.experimental import pallas as pl
from jax.experimental.pallas import tpu as pltpu
from jax.sharding import PartitionSpec as P

BLK = 512


def group_pairs(nseg, group, shift):
    return [
        (seg + nseg * w, seg + nseg * ((w + shift) % group))
        for seg in range(nseg)
        for w in range(group)
    ]


def next_segment_pairs(nseg, group):
    return [
        (seg + nseg * w, (seg + 1) % nseg + nseg * w)
        for seg in range(nseg)
        for w in range(group)
    ]


def block_terms(query_rows, key_block, values, grad_rows, usable):
    scaling = 1.0 / math.sqrt(query_rows.shape[-1])
    scores = (
        jnp.einsum("cid,cjd->cij", query_rows, key_block, preferred_element_type=jnp.float32)
        * scaling
    )
    scores = jnp.where(usable[:, None, :], scores, -jnp.inf)
    highest = jnp.max(scores, axis=2, keepdims=True)
    weights = jnp.exp(scores - highest)
    shares = weights / jnp.sum(weights, axis=2, keepdims=True)
    shares_low = shares.astype(jnp.bfloat16)
    attended = jnp.einsum(
        "cij,cjd->cid", shares_low, values, preferred_element_type=jnp.float32
    ).astype(jnp.bfloat16)
    attended_wide = lax.optimization_barrier(attended).astype(jnp.float32)
    row_dot = jnp.sum(grad_rows.astype(jnp.float32) * attended_wide, axis=2, keepdims=True)
    grad_probs = jnp.einsum("cid,cjd->cij", grad_rows, values, preferred_element_type=jnp.float32)
    dscore = (shares * (grad_probs - row_dot)).astype(jnp.bfloat16)
    grad_query = (
        jnp.einsum("cij,cjd->cid", dscore, key_block, preferred_element_type=jnp.float32) * scaling
    ).astype(jnp.bfloat16)
    key_terms = (
        jnp.einsum("cij,cid->cjd", dscore, query_rows, preferred_element_type=jnp.float32) * scaling
    )
    value_terms = jnp.einsum(
        "cij,cid->cjd", shares_low, grad_rows, preferred_element_type=jnp.float32
    )
    return attended, grad_query, key_terms, value_terms


def attention_kernel(index_ref, flag_ref, q_ref, g_ref, ko_ref, kw_ref, kp_ref, vo_ref, vw_ref, vp_ref, ad_ref, terms_ref):
    place = pl.program_id(0)
    q = q_ref[0]
    g = g_ref[0]
    keys = (ko_ref[0], kw_ref[0], kp_ref[0])
    values = (vo_ref[0], vw_ref[0], vp_ref[0])
    scaling = 1.0 / math.sqrt(q.shape[-1])
    rows_by_rows = (((1,), (1,)), ((), ()))
    cols_by_cols = (((0,), (0,)), ((), ()))
    scores = [
        lax.dot_general(q, k, rows_by_rows, preferred_element_type=jnp.float32) * scaling
        for k in keys
    ]
    kill = jnp.where(place == 0, flag_ref[0], 0)
    scores[1] = jnp.where(kill > 0, -jnp.inf, scores[1])
    highest = jnp.maximum(
        jnp.maximum(jnp.max(scores[0], axis=1, keepdims=True), jnp.max(scores[1], axis=1, keepdims=True)),
        jnp.max(scores[2], axis=1, keepdims=True),
    )
    weights = [jnp.exp(s - highest) for s in scores]
    total = (
        jnp.sum(weights[0], axis=1, keepdims=True)
        + jnp.sum(weights[1], axis=1, keepdims=True)
        + jnp.sum(weights[2], axis=1, keepdims=True)
    )
    shares = [w / total for w in weights]
    shares_low = [s.astype(jnp.bfloat16) for s in shares]
    attended_wide = jnp.dot(shares_low[0], values[0], preferred_element_type=jnp.float32)
    attended_wide = attended_wide + jnp.dot(shares_low[1], values[1], preferred_element_type=jnp.float32)
    attended_wide = attended_wide + jnp.dot(shares_low[2], values[2], preferred_element_type=jnp.float32)
    attended = attended_wide.astype(jnp.bfloat16)
    ad_ref[0, 0] = attended
    row_dot = jnp.sum(g.astype(jnp.float32) * attended.astype(jnp.float32), axis=1, keepdims=True)
    dq = None
    for part in range(3):
        grad_probs = lax.dot_general(g, values[part], rows_by_rows, preferred_element_type=jnp.float32)
        dscore = (shares[part] * (grad_probs - row_dot)).astype(jnp.bfloat16)
        term = jnp.dot(dscore, keys[part], preferred_element_type=jnp.float32)
        dq = term if dq is None else dq + term
        terms_ref[0, part, 0] = (
            lax.dot_general(dscore, q, cols_by_cols, preferred_element_type=jnp.float32) * scaling
        )
        terms_ref[0, part, 1] = lax.dot_general(
            shares_low[part], g, cols_by_cols, preferred_element_type=jnp.float32
        )
    ad_ref[0, 1] = (dq * scaling).astype(jnp.bfloat16)


def fused_terms(parity, q_rows, g_rows, k_all, v_all, k_window, v_window, partner_index, first_masked):
    places, rows, width = q_rows.shape
    row_spec = pl.BlockSpec((1, rows, width), lambda p, idx, flag: (p, 0, 0))
    own_spec = pl.BlockSpec((1, rows, width), lambda p, idx, flag: (2 * p + parity, 0, 0))
    partner_spec = pl.BlockSpec((1, rows, width), lambda p, idx, flag: (idx[p], 0, 0))
    if parity:
        window_spec = pl.BlockSpec((1, rows, width), lambda p, idx, flag: (2 * p, 0, 0))
    else:
        window_spec = row_spec
    flops = 36 * places * rows * rows * width
    return pl.pallas_call(
        attention_kernel,
        grid_spec=pltpu.PrefetchScalarGridSpec(
            num_scalar_prefetch=2,
            grid=(places,),
            in_specs=[row_spec, row_spec, own_spec, window_spec, partner_spec, own_spec, window_spec, partner_spec],
            out_specs=[
                pl.BlockSpec((1, 2, rows, width), lambda p, idx, flag: (p, 0, 0, 0)),
                pl.BlockSpec((1, 3, 2, rows, width), lambda p, idx, flag: (p, 0, 0, 0, 0)),
            ],
        ),
        out_shape=[
            jax.ShapeDtypeStruct((places, 2, rows, width), jnp.bfloat16),
            jax.ShapeDtypeStruct((places, 3, 2, rows, width), jnp.float32),
        ],
        cost_estimate=pl.CostEstimate(
            flops=flops,
            transcendentals=3 * places * rows * rows,
            bytes_accessed=places * rows * width * 60,
        ),
    )(partner_index, first_masked, q_rows, g_rows, k_all, k_window, k_all, v_all, v_window, v_all)


def interleave(even, odd):
    return jnp.stack([even, odd], axis=1).reshape((-1,) + even.shape[1:])


def pick(tree, index):
    return jax.tree.map(lambda x: lax.dynamic_index_in_dim(x, index, axis=0, keepdims=False), tree)


def gather_group(x, within, nseg, group):
    received = [pick(x, within)]
    for shift in range(1, group):
        received.append(lax.ppermute(pick(x, (within + shift) % group), "seq", group_pairs(nseg, group, shift)))
    order = (within - jnp.arange(group, dtype=jnp.int32)) % group
    return jax.tree.map(lambda *r: jnp.take(jnp.stack(r), order, axis=0), *received)


def scatter_group(y, within, nseg, group):
    returned = [pick(y, within)]
    for shift in range(1, group):
        returned.append(
            lax.ppermute(pick(y, (within - shift) % group), "seq", group_pairs(nseg, group, group - shift))
        )
    order = (jnp.arange(group, dtype=jnp.int32) - within) % group
    return jax.tree.map(lambda *r: jnp.take(jnp.stack(r), order, axis=0), *returned)


def body(queries, key_rows, value_rows, grad_out, partner_pos):
    heads, row_count, width = queries.shape
    blocks = row_count // BLK
    places = partner_pos.shape[2]
    group = places // blocks
    if heads != group or blocks != 2:
        raise ValueError("layout mismatch")
    nseg = lax.axis_size("seq") // group
    device = lax.axis_index("seq")
    segment = device % nseg
    within = device // nseg

    def split(x):
        return x.reshape(heads, blocks, BLK, width)

    q4, g4, k4, v4 = split(queries), split(grad_out), split(key_rows), split(value_rows)
    k_local, v_local = gather_group((k4, v4), within, nseg, group)
    k_all = k_local.reshape(places, BLK, width)
    v_all = v_local.reshape(places, BLK, width)
    k_all, v_all, q_odd_send, g_odd_send = lax.optimization_barrier((k_all, v_all, q4[:, 1], g4[:, 1]))
    q_odd, g_odd = gather_group((q_odd_send, g_odd_send), within, nseg, group)
    q_odd, g_odd, q_even_send, g_even_send = lax.optimization_barrier((q_odd, g_odd, q4[:, 0], g4[:, 0]))
    q_even, g_even = gather_group((q_even_send, g_even_send), within, nseg, group)

    odd_kv = jnp.stack([k_all[1::2], v_all[1::2]], axis=1)
    odd_send = jnp.where(segment == nseg - 1, jnp.roll(odd_kv, 1, axis=0), odd_kv)
    window_kv = lax.ppermute(odd_send, "seq", next_segment_pairs(nseg, group))

    my_partners = lax.dynamic_index_in_dim(
        lax.dynamic_index_in_dim(partner_pos, within, axis=0, keepdims=False),
        segment,
        axis=0,
        keepdims=False,
    )
    no_mask = jnp.zeros((1,), jnp.int32)
    ad_odd, terms_odd = fused_terms(
        1, q_odd, g_odd, k_all, v_all, k_all, v_all, my_partners[1::2], no_mask
    )
    sent_odd = scatter_group(ad_odd, within, nseg, group)

    first_masked = (segment == 0).astype(jnp.int32).reshape(1)
    ad_even, terms_even = fused_terms(
        0, q_even, g_even, k_all, v_all, window_kv[:, 0], window_kv[:, 1], my_partners[0::2], first_masked
    )

    ret = terms_even[:, 1]
    ret = jnp.where(segment == 0, jnp.roll(ret, -1, axis=0), ret)
    back_pairs = [(b, a) for a, b in next_segment_pairs(nseg, group)]
    window_back = lax.ppermute(ret, "seq", back_pairs)

    place_ids = jnp.arange(places, dtype=jnp.int32)
    hits = my_partners[None, :] == place_ids[:, None]
    inverse = jnp.sum(jnp.where(hits, place_ids[None, :], 0), axis=1)
    slot = (inverse % 2) * (places // 2) + inverse // 2
    partner_terms = jnp.concatenate([terms_even[:, 2], terms_odd[:, 2]], axis=0)
    partner_even = jnp.take(partner_terms, slot[0::2], axis=0)
    partner_odd = jnp.take(partner_terms, slot[1::2], axis=0)
    grads_even = (terms_even[:, 0] + terms_odd[:, 1] + partner_even).astype(jnp.bfloat16)
    sent_even = scatter_group((ad_even, grads_even), within, nseg, group)
    grads_odd = (terms_odd[:, 0] + window_back + partner_odd).astype(jnp.bfloat16)
    sent_last = scatter_group(grads_odd, within, nseg, group)

    shape = (heads, row_count, width)

    def joined(even, odd):
        return jnp.stack([even, odd], axis=1).reshape(shape)

    ad_e, grads_e = sent_even
    return (
        joined(ad_e[:, 0], sent_odd[:, 0]),
        joined(ad_e[:, 1], sent_odd[:, 1]),
        joined(grads_e[:, 0], sent_last[:, 0]),
        joined(grads_e[:, 1], sent_last[:, 1]),
    )


def solution(mesh):
    return jax.shard_map(
        body,
        mesh=mesh,
        in_specs=(
            P("head", "seq", None),
            P("head", "seq", None),
            P("head", "seq", None),
            P("head", "seq", None),
            P("head", None, None),
        ),
        out_specs=(
            P("head", "seq", None),
            P("head", "seq", None),
            P("head", "seq", None),
            P("head", "seq", None),
        ),
        check_vma=False,
    )
```

```python
import math

import jax
import jax.numpy as jnp
from jax import lax
from jax.experimental import pallas as pl
from jax.experimental.pallas import tpu as pltpu
from jax.sharding import Mesh, PartitionSpec as P

BLK = 512
GROUP = 4


def group_pairs(nseg, group, shift):
    return [
        (seg + nseg * w, seg + nseg * ((w + shift) % group))
        for seg in range(nseg)
        for w in range(group)
    ]


def next_segment_pairs(nseg, group):
    return [
        (seg + nseg * w, (seg + 1) % nseg + nseg * w)
        for seg in range(nseg)
        for w in range(group)
    ]


def block_terms(query_rows, key_block, values, grad_rows, usable):
    scaling = 1.0 / math.sqrt(query_rows.shape[-1])
    scores = (
        jnp.einsum("cid,cjd->cij", query_rows, key_block, preferred_element_type=jnp.float32)
        * scaling
    )
    scores = jnp.where(usable[:, None, :], scores, -jnp.inf)
    highest = jnp.max(scores, axis=2, keepdims=True)
    weights = jnp.exp(scores - highest)
    shares = weights / jnp.sum(weights, axis=2, keepdims=True)
    shares_low = shares.astype(jnp.bfloat16)
    attended = jnp.einsum(
        "cij,cjd->cid", shares_low, values, preferred_element_type=jnp.float32
    ).astype(jnp.bfloat16)
    attended_wide = lax.optimization_barrier(attended).astype(jnp.float32)
    row_dot = jnp.sum(grad_rows.astype(jnp.float32) * attended_wide, axis=2, keepdims=True)
    grad_probs = jnp.einsum("cid,cjd->cij", grad_rows, values, preferred_element_type=jnp.float32)
    dscore = (shares * (grad_probs - row_dot)).astype(jnp.bfloat16)
    grad_query = (
        jnp.einsum("cij,cjd->cid", dscore, key_block, preferred_element_type=jnp.float32) * scaling
    ).astype(jnp.bfloat16)
    key_terms = (
        jnp.einsum("cij,cid->cjd", dscore, query_rows, preferred_element_type=jnp.float32) * scaling
    )
    value_terms = jnp.einsum(
        "cij,cid->cjd", shares_low, grad_rows, preferred_element_type=jnp.float32
    )
    return attended, grad_query, key_terms, value_terms


def attention_kernel(index_ref, flag_ref, q_ref, g_ref, ko_ref, kw_ref, kp_ref, vo_ref, vw_ref, vp_ref, ad_ref, terms_ref):
    place = pl.program_id(0)
    q = q_ref[0]
    g = g_ref[0]
    keys = (ko_ref[0], kw_ref[0], kp_ref[0])
    values = (vo_ref[0], vw_ref[0], vp_ref[0])
    scaling = 1.0 / math.sqrt(q.shape[-1])
    rows_by_rows = (((1,), (1,)), ((), ()))
    cols_by_cols = (((0,), (0,)), ((), ()))
    scores = [
        lax.dot_general(q, k, rows_by_rows, preferred_element_type=jnp.float32) * scaling
        for k in keys
    ]
    kill = jnp.where(place == 0, flag_ref[0], 0)
    scores[1] = jnp.where(kill > 0, -jnp.inf, scores[1])
    highest = jnp.maximum(
        jnp.maximum(jnp.max(scores[0], axis=1, keepdims=True), jnp.max(scores[1], axis=1, keepdims=True)),
        jnp.max(scores[2], axis=1, keepdims=True),
    )
    weights = [jnp.exp(s - highest) for s in scores]
    total = (
        jnp.sum(weights[0], axis=1, keepdims=True)
        + jnp.sum(weights[1], axis=1, keepdims=True)
        + jnp.sum(weights[2], axis=1, keepdims=True)
    )
    shares = [w / total for w in weights]
    shares_low = [s.astype(jnp.bfloat16) for s in shares]
    attended_wide = jnp.dot(shares_low[0], values[0], preferred_element_type=jnp.float32)
    attended_wide = attended_wide + jnp.dot(shares_low[1], values[1], preferred_element_type=jnp.float32)
    attended_wide = attended_wide + jnp.dot(shares_low[2], values[2], preferred_element_type=jnp.float32)
    attended = attended_wide.astype(jnp.bfloat16)
    ad_ref[0, 0] = attended
    row_dot = jnp.sum(g.astype(jnp.float32) * attended.astype(jnp.float32), axis=1, keepdims=True)
    dq = None
    for part in range(3):
        grad_probs = lax.dot_general(g, values[part], rows_by_rows, preferred_element_type=jnp.float32)
        dscore = (shares[part] * (grad_probs - row_dot)).astype(jnp.bfloat16)
        term = jnp.dot(dscore, keys[part], preferred_element_type=jnp.float32)
        dq = term if dq is None else dq + term
        terms_ref[0, part, 0] = (
            lax.dot_general(dscore, q, cols_by_cols, preferred_element_type=jnp.float32) * scaling
        )
        terms_ref[0, part, 1] = lax.dot_general(
            shares_low[part], g, cols_by_cols, preferred_element_type=jnp.float32
        )
    ad_ref[0, 1] = (dq * scaling).astype(jnp.bfloat16)


def fused_terms(parity, q_rows, g_rows, k_all, v_all, k_window, v_window, partner_index, first_masked):
    places, rows, width = q_rows.shape
    row_spec = pl.BlockSpec((1, rows, width), lambda p, idx, flag: (p, 0, 0))
    own_spec = pl.BlockSpec((1, rows, width), lambda p, idx, flag: (2 * p + parity, 0, 0))
    partner_spec = pl.BlockSpec((1, rows, width), lambda p, idx, flag: (idx[p], 0, 0))
    if parity:
        window_spec = pl.BlockSpec((1, rows, width), lambda p, idx, flag: (2 * p, 0, 0))
    else:
        window_spec = row_spec
    flops = 36 * places * rows * rows * width
    return pl.pallas_call(
        attention_kernel,
        grid_spec=pltpu.PrefetchScalarGridSpec(
            num_scalar_prefetch=2,
            grid=(places,),
            in_specs=[row_spec, row_spec, own_spec, window_spec, partner_spec, own_spec, window_spec, partner_spec],
            out_specs=[
                pl.BlockSpec((1, 2, rows, width), lambda p, idx, flag: (p, 0, 0, 0)),
                pl.BlockSpec((1, 3, 2, rows, width), lambda p, idx, flag: (p, 0, 0, 0, 0)),
            ],
        ),
        out_shape=[
            jax.ShapeDtypeStruct((places, 2, rows, width), jnp.bfloat16),
            jax.ShapeDtypeStruct((places, 3, 2, rows, width), jnp.float32),
        ],
        cost_estimate=pl.CostEstimate(
            flops=flops,
            transcendentals=3 * places * rows * rows,
            bytes_accessed=places * rows * width * 60,
        ),
    )(partner_index, first_masked, q_rows, g_rows, k_all, k_window, k_all, v_all, v_window, v_all)


def interleave(even, odd):
    return jnp.stack([even, odd], axis=1).reshape((-1,) + even.shape[1:])


def exchange(tree):
    return jax.tree.map(lambda x: lax.all_to_all(x, "within", 0, 0), tree)


def segment_pairs(nseg, step):
    return [(seg, (seg + step) % nseg) for seg in range(nseg)]


def body(queries, key_rows, value_rows, grad_out, partner_pos):
    heads, row_count, width = queries.shape
    blocks = row_count // BLK
    places = partner_pos.shape[2]
    group = places // blocks
    if heads != group or blocks != 2:
        raise ValueError("layout mismatch")
    if lax.axis_size("within") != group:
        raise ValueError("group mismatch")
    nseg = lax.axis_size("segment")
    segment = lax.axis_index("segment")

    def split(x):
        return x.reshape(heads, blocks, BLK, width)

    q4, g4, k4, v4 = split(queries), split(grad_out), split(key_rows), split(value_rows)
    k_local, v_local = exchange((k4, v4))
    k_all = k_local.reshape(places, BLK, width)
    v_all = v_local.reshape(places, BLK, width)
    k_all, v_all, q_odd_send, g_odd_send = lax.optimization_barrier((k_all, v_all, q4[:, 1], g4[:, 1]))
    q_odd, g_odd = exchange((q_odd_send, g_odd_send))
    q_odd, g_odd, q_even_send, g_even_send = lax.optimization_barrier((q_odd, g_odd, q4[:, 0], g4[:, 0]))
    q_even, g_even = exchange((q_even_send, g_even_send))

    odd_kv = jnp.stack([k_all[1::2], v_all[1::2]], axis=1)
    odd_send = jnp.where(segment == nseg - 1, jnp.roll(odd_kv, 1, axis=0), odd_kv)
    window_kv = lax.ppermute(odd_send, "segment", segment_pairs(nseg, 1))

    within = lax.axis_index("within")
    my_partners = lax.dynamic_index_in_dim(
        lax.dynamic_index_in_dim(partner_pos, within, axis=0, keepdims=False),
        segment,
        axis=0,
        keepdims=False,
    )
    no_mask = jnp.zeros((1,), jnp.int32)
    ad_odd, terms_odd = fused_terms(
        1, q_odd, g_odd, k_all, v_all, k_all, v_all, my_partners[1::2], no_mask
    )
    sent_odd = exchange(ad_odd)

    first_masked = (segment == 0).astype(jnp.int32).reshape(1)
    ad_even, terms_even = fused_terms(
        0, q_even, g_even, k_all, v_all, window_kv[:, 0], window_kv[:, 1], my_partners[0::2], first_masked
    )

    ret = terms_even[:, 1]
    ret = jnp.where(segment == 0, jnp.roll(ret, -1, axis=0), ret)
    window_back = lax.ppermute(ret, "segment", segment_pairs(nseg, nseg - 1))

    place_ids = jnp.arange(places, dtype=jnp.int32)
    hits = my_partners[None, :] == place_ids[:, None]
    inverse = jnp.sum(jnp.where(hits, place_ids[None, :], 0), axis=1)
    slot = (inverse % 2) * (places // 2) + inverse // 2
    partner_terms = jnp.concatenate([terms_even[:, 2], terms_odd[:, 2]], axis=0)
    partner_even = jnp.take(partner_terms, slot[0::2], axis=0)
    partner_odd = jnp.take(partner_terms, slot[1::2], axis=0)
    grads_even = (terms_even[:, 0] + terms_odd[:, 1] + partner_even).astype(jnp.bfloat16)
    sent_even = exchange((ad_even, grads_even))
    grads_odd = (terms_odd[:, 0] + window_back + partner_odd).astype(jnp.bfloat16)
    sent_last = exchange(grads_odd)

    shape = (heads, row_count, width)

    def joined(even, odd):
        return jnp.stack([even, odd], axis=1).reshape(shape)

    ad_e, grads_e = sent_even
    return (
        joined(ad_e[:, 0], sent_odd[:, 0]),
        joined(ad_e[:, 1], sent_odd[:, 1]),
        joined(grads_e[:, 0], sent_last[:, 0]),
        joined(grads_e[:, 1], sent_last[:, 1]),
    )


def solution(mesh):
    devices = mesh.devices
    grouped = Mesh(
        devices.reshape((GROUP, devices.shape[0] // GROUP) + devices.shape[1:]),
        ("within", "segment", "head"),
    )
    rows = P("head", ("within", "segment"), None)
    return jax.shard_map(
        body,
        mesh=grouped,
        in_specs=(rows, rows, rows, rows, P("head", None, None)),
        out_specs=(rows, rows, rows, rows),
        check_vma=False,
    )
```

```python
import math

import jax
import jax.numpy as jnp
from jax import lax
from jax.experimental import pallas as pl
from jax.experimental.pallas import tpu as pltpu
from jax.sharding import PartitionSpec as P

BLK = 512


def group_pairs(nseg, group, shift):
    return [
        (seg + nseg * w, seg + nseg * ((w + shift) % group))
        for seg in range(nseg)
        for w in range(group)
    ]


def next_segment_pairs(nseg, group):
    return [
        (seg + nseg * w, (seg + 1) % nseg + nseg * w)
        for seg in range(nseg)
        for w in range(group)
    ]


def block_terms(query_rows, key_block, values, grad_rows, usable):
    scaling = 1.0 / math.sqrt(query_rows.shape[-1])
    scores = (
        jnp.einsum("cid,cjd->cij", query_rows, key_block, preferred_element_type=jnp.float32)
        * scaling
    )
    scores = jnp.where(usable[:, None, :], scores, -jnp.inf)
    highest = jnp.max(scores, axis=2, keepdims=True)
    weights = jnp.exp(scores - highest)
    shares = weights / jnp.sum(weights, axis=2, keepdims=True)
    shares_low = shares.astype(jnp.bfloat16)
    attended = jnp.einsum(
        "cij,cjd->cid", shares_low, values, preferred_element_type=jnp.float32
    ).astype(jnp.bfloat16)
    attended_wide = lax.optimization_barrier(attended).astype(jnp.float32)
    row_dot = jnp.sum(grad_rows.astype(jnp.float32) * attended_wide, axis=2, keepdims=True)
    grad_probs = jnp.einsum("cid,cjd->cij", grad_rows, values, preferred_element_type=jnp.float32)
    dscore = (shares * (grad_probs - row_dot)).astype(jnp.bfloat16)
    grad_query = (
        jnp.einsum("cij,cjd->cid", dscore, key_block, preferred_element_type=jnp.float32) * scaling
    ).astype(jnp.bfloat16)
    key_terms = (
        jnp.einsum("cij,cid->cjd", dscore, query_rows, preferred_element_type=jnp.float32) * scaling
    )
    value_terms = jnp.einsum(
        "cij,cid->cjd", shares_low, grad_rows, preferred_element_type=jnp.float32
    )
    return attended, grad_query, key_terms, value_terms


def attention_kernel(index_ref, flag_ref, q_ref, g_ref, ko_ref, kw_ref, kp_ref, vo_ref, vw_ref, vp_ref, ad_ref, own_ref, win_ref, par_ref):
    place = pl.program_id(0)
    q = q_ref[0]
    g = g_ref[0]
    keys = (ko_ref[0], kw_ref[0], kp_ref[0])
    values = (vo_ref[0], vw_ref[0], vp_ref[0])
    scaling = 1.0 / math.sqrt(q.shape[-1])
    rows_by_rows = (((1,), (1,)), ((), ()))
    cols_by_cols = (((0,), (0,)), ((), ()))
    scores = [
        lax.dot_general(q, k, rows_by_rows, preferred_element_type=jnp.float32) * scaling
        for k in keys
    ]
    kill = jnp.where(place == 0, flag_ref[0], 0)
    scores[1] = jnp.where(kill > 0, -jnp.inf, scores[1])
    highest = jnp.maximum(
        jnp.maximum(jnp.max(scores[0], axis=1, keepdims=True), jnp.max(scores[1], axis=1, keepdims=True)),
        jnp.max(scores[2], axis=1, keepdims=True),
    )
    weights = [jnp.exp(s - highest) for s in scores]
    total = (
        jnp.sum(weights[0], axis=1, keepdims=True)
        + jnp.sum(weights[1], axis=1, keepdims=True)
        + jnp.sum(weights[2], axis=1, keepdims=True)
    )
    shares = [w / total for w in weights]
    shares_low = [s.astype(jnp.bfloat16) for s in shares]
    attended_wide = jnp.dot(shares_low[0], values[0], preferred_element_type=jnp.float32)
    attended_wide = attended_wide + jnp.dot(shares_low[1], values[1], preferred_element_type=jnp.float32)
    attended_wide = attended_wide + jnp.dot(shares_low[2], values[2], preferred_element_type=jnp.float32)
    attended = attended_wide.astype(jnp.bfloat16)
    ad_ref[0, 0] = attended
    row_dot = jnp.sum(g.astype(jnp.float32) * attended.astype(jnp.float32), axis=1, keepdims=True)
    dq = None
    for part in range(3):
        grad_probs = lax.dot_general(g, values[part], rows_by_rows, preferred_element_type=jnp.float32)
        dscore = (shares[part] * (grad_probs - row_dot)).astype(jnp.bfloat16)
        term = jnp.dot(dscore, keys[part], preferred_element_type=jnp.float32)
        dq = term if dq is None else dq + term
        out_ref = (own_ref, win_ref, par_ref)[part]
        out_ref[0, 0] = (
            lax.dot_general(dscore, q, cols_by_cols, preferred_element_type=jnp.float32) * scaling
        )
        out_ref[0, 1] = lax.dot_general(
            shares_low[part], g, cols_by_cols, preferred_element_type=jnp.float32
        )
    ad_ref[0, 1] = (dq * scaling).astype(jnp.bfloat16)


def fused_terms(parity, q_rows, g_rows, k_all, v_all, k_window, v_window, partner_index, first_masked):
    places, rows, width = q_rows.shape
    row_spec = pl.BlockSpec((1, rows, width), lambda p, idx, flag: (p, 0, 0))
    own_spec = pl.BlockSpec((1, rows, width), lambda p, idx, flag: (2 * p + parity, 0, 0))
    partner_spec = pl.BlockSpec((1, rows, width), lambda p, idx, flag: (idx[p], 0, 0))
    if parity:
        window_spec = pl.BlockSpec((1, rows, width), lambda p, idx, flag: (2 * p, 0, 0))
    else:
        window_spec = row_spec
    flops = 36 * places * rows * rows * width
    return pl.pallas_call(
        attention_kernel,
        grid_spec=pltpu.PrefetchScalarGridSpec(
            num_scalar_prefetch=2,
            grid=(places,),
            in_specs=[row_spec, row_spec, own_spec, window_spec, partner_spec, own_spec, window_spec, partner_spec],
            out_specs=[pl.BlockSpec((1, 2, rows, width), lambda p, idx, flag: (p, 0, 0, 0))] * 4,
        ),
        out_shape=[jax.ShapeDtypeStruct((places, 2, rows, width), jnp.bfloat16)]
        + [jax.ShapeDtypeStruct((places, 2, rows, width), jnp.float32)] * 3,
        cost_estimate=pl.CostEstimate(
            flops=flops,
            transcendentals=3 * places * rows * rows,
            bytes_accessed=places * rows * width * 60,
        ),
    )(partner_index, first_masked, q_rows, g_rows, k_all, k_window, k_all, v_all, v_window, v_all)


def interleave(even, odd):
    return jnp.stack([even, odd], axis=1).reshape((-1,) + even.shape[1:])


def pick(tree, index):
    return jax.tree.map(lambda x: lax.dynamic_index_in_dim(x, index, axis=0, keepdims=False), tree)


def gather_group(x, within, nseg, group):
    received = [pick(x, within)]
    for shift in range(1, group):
        received.append(lax.ppermute(pick(x, (within + shift) % group), "seq", group_pairs(nseg, group, shift)))
    order = (within - jnp.arange(group, dtype=jnp.int32)) % group
    return jax.tree.map(lambda *r: jnp.take(jnp.stack(r), order, axis=0), *received)


def scatter_group(y, within, nseg, group):
    returned = [pick(y, within)]
    for shift in range(1, group):
        returned.append(
            lax.ppermute(pick(y, (within - shift) % group), "seq", group_pairs(nseg, group, group - shift))
        )
    order = (jnp.arange(group, dtype=jnp.int32) - within) % group
    return jax.tree.map(lambda *r: jnp.take(jnp.stack(r), order, axis=0), *returned)


def body(queries, key_rows, value_rows, grad_out, partner_pos):
    heads, row_count, width = queries.shape
    blocks = row_count // BLK
    places = partner_pos.shape[2]
    group = places // blocks
    if heads != group or blocks != 2:
        raise ValueError("layout mismatch")
    nseg = lax.axis_size("seq") // group
    device = lax.axis_index("seq")
    segment = device % nseg
    within = device // nseg

    def split(x):
        return x.reshape(heads, blocks, BLK, width)

    q4, g4, k4, v4 = split(queries), split(grad_out), split(key_rows), split(value_rows)
    k_local, v_local = gather_group((k4, v4), within, nseg, group)
    k_all = k_local.reshape(places, BLK, width)
    v_all = v_local.reshape(places, BLK, width)
    k_all, v_all, q_odd_send, g_odd_send = lax.optimization_barrier((k_all, v_all, q4[:, 1], g4[:, 1]))
    q_odd, g_odd = gather_group((q_odd_send, g_odd_send), within, nseg, group)
    q_odd, g_odd, q_even_send, g_even_send = lax.optimization_barrier((q_odd, g_odd, q4[:, 0], g4[:, 0]))
    q_even, g_even = gather_group((q_even_send, g_even_send), within, nseg, group)

    odd_kv = jnp.stack([k_all[1::2], v_all[1::2]], axis=1)
    odd_send = jnp.where(segment == nseg - 1, jnp.roll(odd_kv, 1, axis=0), odd_kv)
    window_kv = lax.ppermute(odd_send, "seq", next_segment_pairs(nseg, group))

    my_partners = lax.dynamic_index_in_dim(
        lax.dynamic_index_in_dim(partner_pos, within, axis=0, keepdims=False),
        segment,
        axis=0,
        keepdims=False,
    )
    no_mask = jnp.zeros((1,), jnp.int32)
    ad_odd, own_odd, win_odd, par_odd = fused_terms(
        1, q_odd, g_odd, k_all, v_all, k_all, v_all, my_partners[1::2], no_mask
    )
    sent_odd = scatter_group(ad_odd, within, nseg, group)

    first_masked = (segment == 0).astype(jnp.int32).reshape(1)
    ad_even, own_even, win_even, par_even = fused_terms(
        0, q_even, g_even, k_all, v_all, window_kv[:, 0], window_kv[:, 1], my_partners[0::2], first_masked
    )

    ret = win_even
    ret = jnp.where(segment == 0, jnp.roll(ret, -1, axis=0), ret)
    back_pairs = [(b, a) for a, b in next_segment_pairs(nseg, group)]
    window_back = lax.ppermute(ret, "seq", back_pairs)

    place_ids = jnp.arange(places, dtype=jnp.int32)
    hits = my_partners[None, :] == place_ids[:, None]
    inverse = jnp.sum(jnp.where(hits, place_ids[None, :], 0), axis=1)
    slot = (inverse % 2) * (places // 2) + inverse // 2
    partner_terms = jnp.concatenate([par_even, par_odd], axis=0)
    partner_even = jnp.take(partner_terms, slot[0::2], axis=0)
    partner_odd = jnp.take(partner_terms, slot[1::2], axis=0)
    grads_even = (own_even + win_odd + partner_even).astype(jnp.bfloat16)
    sent_even = scatter_group((ad_even, grads_even), within, nseg, group)
    grads_odd = (own_odd + window_back + partner_odd).astype(jnp.bfloat16)
    sent_last = scatter_group(grads_odd, within, nseg, group)

    shape = (heads, row_count, width)

    def joined(even, odd):
        return jnp.stack([even, odd], axis=1).reshape(shape)

    ad_e, grads_e = sent_even
    return (
        joined(ad_e[:, 0], sent_odd[:, 0]),
        joined(ad_e[:, 1], sent_odd[:, 1]),
        joined(grads_e[:, 0], sent_last[:, 0]),
        joined(grads_e[:, 1], sent_last[:, 1]),
    )


def solution(mesh):
    return jax.shard_map(
        body,
        mesh=mesh,
        in_specs=(
            P("head", "seq", None),
            P("head", "seq", None),
            P("head", "seq", None),
            P("head", "seq", None),
            P("head", None, None),
        ),
        out_specs=(
            P("head", "seq", None),
            P("head", "seq", None),
            P("head", "seq", None),
            P("head", "seq", None),
        ),
        check_vma=False,
    )
```

```python
import math

import jax
import jax.numpy as jnp
from jax import lax
from jax.experimental import pallas as pl
from jax.experimental.pallas import tpu as pltpu
from jax.sharding import PartitionSpec as P

BLK = 512


def group_pairs(nseg, group, shift):
    return [
        (seg + nseg * w, seg + nseg * ((w + shift) % group))
        for seg in range(nseg)
        for w in range(group)
    ]


def next_segment_pairs(nseg, group):
    return [
        (seg + nseg * w, (seg + 1) % nseg + nseg * w)
        for seg in range(nseg)
        for w in range(group)
    ]


def block_terms(query_rows, key_block, values, grad_rows, usable):
    scaling = 1.0 / math.sqrt(query_rows.shape[-1])
    scores = (
        jnp.einsum("cid,cjd->cij", query_rows, key_block, preferred_element_type=jnp.float32)
        * scaling
    )
    scores = jnp.where(usable[:, None, :], scores, -jnp.inf)
    highest = jnp.max(scores, axis=2, keepdims=True)
    weights = jnp.exp(scores - highest)
    shares = weights / jnp.sum(weights, axis=2, keepdims=True)
    shares_low = shares.astype(jnp.bfloat16)
    attended = jnp.einsum(
        "cij,cjd->cid", shares_low, values, preferred_element_type=jnp.float32
    ).astype(jnp.bfloat16)
    attended_wide = lax.optimization_barrier(attended).astype(jnp.float32)
    row_dot = jnp.sum(grad_rows.astype(jnp.float32) * attended_wide, axis=2, keepdims=True)
    grad_probs = jnp.einsum("cid,cjd->cij", grad_rows, values, preferred_element_type=jnp.float32)
    dscore = (shares * (grad_probs - row_dot)).astype(jnp.bfloat16)
    grad_query = (
        jnp.einsum("cij,cjd->cid", dscore, key_block, preferred_element_type=jnp.float32) * scaling
    ).astype(jnp.bfloat16)
    key_terms = (
        jnp.einsum("cij,cid->cjd", dscore, query_rows, preferred_element_type=jnp.float32) * scaling
    )
    value_terms = jnp.einsum(
        "cij,cid->cjd", shares_low, grad_rows, preferred_element_type=jnp.float32
    )
    return attended, grad_query, key_terms, value_terms


def attention_kernel(index_ref, flag_ref, q_ref, g_ref, ko_ref, kw_ref, kp_ref, vo_ref, vw_ref, vp_ref, ad_ref, own_ref, win_ref, par_ref):
    place = pl.program_id(0)
    q = q_ref[0]
    g = g_ref[0]
    keys = (ko_ref[0], kw_ref[0], kp_ref[0])
    values = (vo_ref[0], vw_ref[0], vp_ref[0])
    scaling = 1.0 / math.sqrt(q.shape[-1])
    rows_by_rows = (((1,), (1,)), ((), ()))
    cols_by_cols = (((0,), (0,)), ((), ()))
    scores = [
        lax.dot_general(q, k, rows_by_rows, preferred_element_type=jnp.float32) * scaling
        for k in keys
    ]
    kill = jnp.where(place == 0, flag_ref[0], 0)
    scores[1] = jnp.where(kill > 0, -jnp.inf, scores[1])
    highest = jnp.maximum(
        jnp.maximum(jnp.max(scores[0], axis=1, keepdims=True), jnp.max(scores[1], axis=1, keepdims=True)),
        jnp.max(scores[2], axis=1, keepdims=True),
    )
    weights = [jnp.exp(s - highest) for s in scores]
    total = (
        jnp.sum(weights[0], axis=1, keepdims=True)
        + jnp.sum(weights[1], axis=1, keepdims=True)
        + jnp.sum(weights[2], axis=1, keepdims=True)
    )
    shares = [w / total for w in weights]
    shares_low = [s.astype(jnp.bfloat16) for s in shares]
    attended_wide = jnp.dot(shares_low[0], values[0], preferred_element_type=jnp.float32)
    attended_wide = attended_wide + jnp.dot(shares_low[1], values[1], preferred_element_type=jnp.float32)
    attended_wide = attended_wide + jnp.dot(shares_low[2], values[2], preferred_element_type=jnp.float32)
    attended = attended_wide.astype(jnp.bfloat16)
    ad_ref[0, 0] = attended
    row_dot = jnp.sum(g.astype(jnp.float32) * attended.astype(jnp.float32), axis=1, keepdims=True)
    dq = None
    for part in range(3):
        grad_probs = lax.dot_general(g, values[part], rows_by_rows, preferred_element_type=jnp.float32)
        dscore = (shares[part] * (grad_probs - row_dot)).astype(jnp.bfloat16)
        term = jnp.dot(dscore, keys[part], preferred_element_type=jnp.float32)
        dq = term if dq is None else dq + term
        out_ref = (own_ref, win_ref, par_ref)[part]
        out_ref[0, 0] = (
            lax.dot_general(dscore, q, cols_by_cols, preferred_element_type=jnp.float32) * scaling
        )
        out_ref[0, 1] = lax.dot_general(
            shares_low[part], g, cols_by_cols, preferred_element_type=jnp.float32
        )
    ad_ref[0, 1] = (dq * scaling).astype(jnp.bfloat16)


def fused_terms(parity, q_rows, g_rows, k_all, v_all, k_window, v_window, partner_index, first_masked):
    places, rows, width = q_rows.shape
    row_spec = pl.BlockSpec((1, rows, width), lambda p, idx, flag: (p, 0, 0))
    own_spec = pl.BlockSpec((1, rows, width), lambda p, idx, flag: (2 * p + parity, 0, 0))
    partner_spec = pl.BlockSpec((1, rows, width), lambda p, idx, flag: (idx[p], 0, 0))
    if parity:
        window_spec = pl.BlockSpec((1, rows, width), lambda p, idx, flag: (2 * p, 0, 0))
    else:
        window_spec = row_spec
    flops = 36 * places * rows * rows * width
    return pl.pallas_call(
        attention_kernel,
        grid_spec=pltpu.PrefetchScalarGridSpec(
            num_scalar_prefetch=2,
            grid=(places,),
            in_specs=[row_spec, row_spec, own_spec, window_spec, partner_spec, own_spec, window_spec, partner_spec],
            out_specs=[pl.BlockSpec((1, 2, rows, width), lambda p, idx, flag: (p, 0, 0, 0))] * 4,
        ),
        out_shape=[jax.ShapeDtypeStruct((places, 2, rows, width), jnp.bfloat16)]
        + [jax.ShapeDtypeStruct((places, 2, rows, width), jnp.float32)] * 3,
        cost_estimate=pl.CostEstimate(
            flops=flops,
            transcendentals=3 * places * rows * rows,
            bytes_accessed=places * rows * width * 60,
        ),
    )(partner_index, first_masked, q_rows, g_rows, k_all, k_window, k_all, v_all, v_window, v_all)


def interleave(even, odd):
    return jnp.stack([even, odd], axis=1).reshape((-1,) + even.shape[1:])


def pick(tree, index):
    return jax.tree.map(lambda x: lax.dynamic_index_in_dim(x, index, axis=0, keepdims=False), tree)


def gather_group(x, within, nseg, group):
    received = [pick(x, within)]
    for shift in range(1, group):
        received.append(lax.ppermute(pick(x, (within + shift) % group), "seq", group_pairs(nseg, group, shift)))

    def place(*pieces):
        out = jnp.zeros((group,) + pieces[0].shape, pieces[0].dtype)
        for shift, piece in enumerate(pieces):
            out = lax.dynamic_update_index_in_dim(out, piece, (within - shift) % group, 0)
        return out

    return jax.tree.map(place, *received)


def scatter_group(y, within, nseg, group):
    returned = [pick(y, within)]
    for shift in range(1, group):
        returned.append(
            lax.ppermute(pick(y, (within - shift) % group), "seq", group_pairs(nseg, group, group - shift))
        )
    return [((within + shift) % group, piece) for shift, piece in enumerate(returned)]


def assemble(even_parts, odd_parts, heads, shape):
    first = even_parts[0][1]
    out = jnp.zeros((heads, 2) + first.shape, first.dtype)
    zero = jnp.zeros((), jnp.int32)
    for column, parts in ((0, even_parts), (1, odd_parts)):
        for head, piece in parts:
            out = lax.dynamic_update_slice(
                out, piece[None, None], (head, jnp.int32(column), zero, zero)
            )
    return out.reshape(shape)


def body(queries, key_rows, value_rows, grad_out, partner_pos):
    heads, row_count, width = queries.shape
    blocks = row_count // BLK
    places = partner_pos.shape[2]
    group = places // blocks
    if heads != group or blocks != 2:
        raise ValueError("layout mismatch")
    nseg = lax.axis_size("seq") // group
    device = lax.axis_index("seq")
    segment = device % nseg
    within = device // nseg

    def split(x):
        return x.reshape(heads, blocks, BLK, width)

    q4, g4, k4, v4 = split(queries), split(grad_out), split(key_rows), split(value_rows)
    k_local, v_local = gather_group((k4, v4), within, nseg, group)
    k_all = k_local.reshape(places, BLK, width)
    v_all = v_local.reshape(places, BLK, width)
    k_all, v_all, q_odd_send, g_odd_send = lax.optimization_barrier((k_all, v_all, q4[:, 1], g4[:, 1]))
    q_odd, g_odd = gather_group((q_odd_send, g_odd_send), within, nseg, group)
    q_odd, g_odd, q_even_send, g_even_send = lax.optimization_barrier((q_odd, g_odd, q4[:, 0], g4[:, 0]))
    q_even, g_even = gather_group((q_even_send, g_even_send), within, nseg, group)

    odd_kv = jnp.stack([k_all[1::2], v_all[1::2]], axis=1)
    odd_send = jnp.where(segment == nseg - 1, jnp.roll(odd_kv, 1, axis=0), odd_kv)
    window_kv = lax.ppermute(odd_send, "seq", next_segment_pairs(nseg, group))

    my_partners = lax.dynamic_index_in_dim(
        lax.dynamic_index_in_dim(partner_pos, within, axis=0, keepdims=False),
        segment,
        axis=0,
        keepdims=False,
    )
    no_mask = jnp.zeros((1,), jnp.int32)
    ad_odd, own_odd, win_odd, par_odd = fused_terms(
        1, q_odd, g_odd, k_all, v_all, k_all, v_all, my_partners[1::2], no_mask
    )
    sent_odd = scatter_group(ad_odd, within, nseg, group)

    first_masked = (segment == 0).astype(jnp.int32).reshape(1)
    ad_even, own_even, win_even, par_even = fused_terms(
        0, q_even, g_even, k_all, v_all, window_kv[:, 0], window_kv[:, 1], my_partners[0::2], first_masked
    )

    ret = win_even
    ret = jnp.where(segment == 0, jnp.roll(ret, -1, axis=0), ret)
    back_pairs = [(b, a) for a, b in next_segment_pairs(nseg, group)]
    window_back = lax.ppermute(ret, "seq", back_pairs)

    place_ids = jnp.arange(places, dtype=jnp.int32)
    hits = my_partners[None, :] == place_ids[:, None]
    inverse = jnp.sum(jnp.where(hits, place_ids[None, :], 0), axis=1)
    slot = (inverse % 2) * (places // 2) + inverse // 2
    partner_terms = jnp.concatenate([par_even, par_odd], axis=0)
    partner_even = jnp.take(partner_terms, slot[0::2], axis=0)
    partner_odd = jnp.take(partner_terms, slot[1::2], axis=0)
    grads_even = (own_even + win_odd + partner_even).astype(jnp.bfloat16)
    sent_even = scatter_group((ad_even, grads_even), within, nseg, group)
    grads_odd = (own_odd + window_back + partner_odd).astype(jnp.bfloat16)
    sent_last = scatter_group(grads_odd, within, nseg, group)

    shape = (heads, row_count, width)

    def column(parts, index, entry=None):
        if entry is None:
            return [(h, piece[index]) for h, piece in parts]
        return [(h, piece[entry][index]) for h, piece in parts]

    return (
        assemble(column(sent_even, 0, 0), column(sent_odd, 0), heads, shape),
        assemble(column(sent_even, 1, 0), column(sent_odd, 1), heads, shape),
        assemble(column(sent_even, 0, 1), column(sent_last, 0), heads, shape),
        assemble(column(sent_even, 1, 1), column(sent_last, 1), heads, shape),
    )


def solution(mesh):
    return jax.shard_map(
        body,
        mesh=mesh,
        in_specs=(
            P("head", "seq", None),
            P("head", "seq", None),
            P("head", "seq", None),
            P("head", "seq", None),
            P("head", None, None),
        ),
        out_specs=(
            P("head", "seq", None),
            P("head", "seq", None),
            P("head", "seq", None),
            P("head", "seq", None),
        ),
        check_vma=False,
    )
```

```python
import math

import jax
import jax.numpy as jnp
from jax import lax
from jax.experimental import pallas as pl
from jax.experimental.pallas import tpu as pltpu
from jax.sharding import PartitionSpec as P

BLK = 512


def group_pairs(nseg, group, shift):
    return [
        (seg + nseg * w, seg + nseg * ((w + shift) % group))
        for seg in range(nseg)
        for w in range(group)
    ]


def next_segment_pairs(nseg, group):
    return [
        (seg + nseg * w, (seg + 1) % nseg + nseg * w)
        for seg in range(nseg)
        for w in range(group)
    ]


def block_terms(query_rows, key_block, values, grad_rows, usable):
    scaling = 1.0 / math.sqrt(query_rows.shape[-1])
    scores = (
        jnp.einsum("cid,cjd->cij", query_rows, key_block, preferred_element_type=jnp.float32)
        * scaling
    )
    scores = jnp.where(usable[:, None, :], scores, -jnp.inf)
    highest = jnp.max(scores, axis=2, keepdims=True)
    weights = jnp.exp(scores - highest)
    shares = weights / jnp.sum(weights, axis=2, keepdims=True)
    shares_low = shares.astype(jnp.bfloat16)
    attended = jnp.einsum(
        "cij,cjd->cid", shares_low, values, preferred_element_type=jnp.float32
    ).astype(jnp.bfloat16)
    attended_wide = lax.optimization_barrier(attended).astype(jnp.float32)
    row_dot = jnp.sum(grad_rows.astype(jnp.float32) * attended_wide, axis=2, keepdims=True)
    grad_probs = jnp.einsum("cid,cjd->cij", grad_rows, values, preferred_element_type=jnp.float32)
    dscore = (shares * (grad_probs - row_dot)).astype(jnp.bfloat16)
    grad_query = (
        jnp.einsum("cij,cjd->cid", dscore, key_block, preferred_element_type=jnp.float32) * scaling
    ).astype(jnp.bfloat16)
    key_terms = (
        jnp.einsum("cij,cid->cjd", dscore, query_rows, preferred_element_type=jnp.float32) * scaling
    )
    value_terms = jnp.einsum(
        "cij,cid->cjd", shares_low, grad_rows, preferred_element_type=jnp.float32
    )
    return attended, grad_query, key_terms, value_terms


def attention_kernel(index_ref, flag_ref, q_ref, g_ref, ko_ref, kw_ref, kp_ref, vo_ref, vw_ref, vp_ref, ad_ref, own_ref, win_ref, par_ref):
    place = pl.program_id(0)
    q = q_ref[0]
    g = g_ref[0]
    keys = (ko_ref[0], kw_ref[0], kp_ref[0])
    values = (vo_ref[0], vw_ref[0], vp_ref[0])
    scaling = 1.0 / math.sqrt(q.shape[-1])
    rows_by_rows = (((1,), (1,)), ((), ()))
    cols_by_cols = (((0,), (0,)), ((), ()))
    scores = [
        lax.dot_general(q, k, rows_by_rows, preferred_element_type=jnp.float32) * scaling
        for k in keys
    ]
    kill = jnp.where(place == 0, flag_ref[0], 0)
    scores[1] = jnp.where(kill > 0, -jnp.inf, scores[1])
    highest = jnp.maximum(
        jnp.maximum(jnp.max(scores[0], axis=1, keepdims=True), jnp.max(scores[1], axis=1, keepdims=True)),
        jnp.max(scores[2], axis=1, keepdims=True),
    )
    weights = [jnp.exp(s - highest) for s in scores]
    total = (
        jnp.sum(weights[0], axis=1, keepdims=True)
        + jnp.sum(weights[1], axis=1, keepdims=True)
        + jnp.sum(weights[2], axis=1, keepdims=True)
    )
    shares = [w / total for w in weights]
    shares_low = [s.astype(jnp.bfloat16) for s in shares]
    attended_wide = jnp.dot(shares_low[0], values[0], preferred_element_type=jnp.float32)
    attended_wide = attended_wide + jnp.dot(shares_low[1], values[1], preferred_element_type=jnp.float32)
    attended_wide = attended_wide + jnp.dot(shares_low[2], values[2], preferred_element_type=jnp.float32)
    attended = attended_wide.astype(jnp.bfloat16)
    ad_ref[0, 0] = attended
    row_dot = jnp.sum(g.astype(jnp.float32) * attended.astype(jnp.float32), axis=1, keepdims=True)
    dq = None
    for part in range(3):
        grad_probs = lax.dot_general(g, values[part], rows_by_rows, preferred_element_type=jnp.float32)
        dscore = (shares[part] * (grad_probs - row_dot)).astype(jnp.bfloat16)
        term = jnp.dot(dscore, keys[part], preferred_element_type=jnp.float32)
        dq = term if dq is None else dq + term
        out_ref = (own_ref, win_ref, par_ref)[part]
        out_ref[0, 0] = (
            lax.dot_general(dscore, q, cols_by_cols, preferred_element_type=jnp.float32) * scaling
        )
        out_ref[0, 1] = lax.dot_general(
            shares_low[part], g, cols_by_cols, preferred_element_type=jnp.float32
        )
    ad_ref[0, 1] = (dq * scaling).astype(jnp.bfloat16)


def fused_terms(parity, q_rows, g_rows, k_all, v_all, k_window, v_window, partner_index, first_masked):
    places, rows, width = q_rows.shape
    row_spec = pl.BlockSpec((1, rows, width), lambda p, idx, flag: (p, 0, 0))
    own_spec = pl.BlockSpec((1, rows, width), lambda p, idx, flag: (2 * p + parity, 0, 0))
    partner_spec = pl.BlockSpec((1, rows, width), lambda p, idx, flag: (idx[p], 0, 0))
    if parity:
        window_spec = pl.BlockSpec((1, rows, width), lambda p, idx, flag: (2 * p, 0, 0))
    else:
        window_spec = row_spec
    flops = 36 * places * rows * rows * width
    return pl.pallas_call(
        attention_kernel,
        grid_spec=pltpu.PrefetchScalarGridSpec(
            num_scalar_prefetch=2,
            grid=(places,),
            in_specs=[row_spec, row_spec, own_spec, window_spec, partner_spec, own_spec, window_spec, partner_spec],
            out_specs=[pl.BlockSpec((1, 2, rows, width), lambda p, idx, flag: (p, 0, 0, 0))] * 4,
        ),
        out_shape=[jax.ShapeDtypeStruct((places, 2, rows, width), jnp.bfloat16)]
        + [jax.ShapeDtypeStruct((places, 2, rows, width), jnp.float32)] * 3,
        cost_estimate=pl.CostEstimate(
            flops=flops,
            transcendentals=3 * places * rows * rows,
            bytes_accessed=places * rows * width * 60,
        ),
    )(partner_index, first_masked, q_rows, g_rows, k_all, k_window, k_all, v_all, v_window, v_all)


def interleave(even, odd):
    return jnp.stack([even, odd], axis=1).reshape((-1,) + even.shape[1:])


def pick(tree, index):
    return jax.tree.map(lambda x: lax.dynamic_index_in_dim(x, index, axis=0, keepdims=False), tree)


def gather_group(x, within, nseg, group):
    received = [pick(x, within)]
    for shift in range(1, group):
        received.append(lax.ppermute(pick(x, (within + shift) % group), "seq", group_pairs(nseg, group, shift)))

    def place(*pieces):
        out = jnp.zeros((group,) + pieces[0].shape, pieces[0].dtype)
        for shift, piece in enumerate(pieces):
            out = lax.dynamic_update_index_in_dim(out, piece, (within - shift) % group, 0)
        return out

    return jax.tree.map(place, *received)


def scatter_group(y, within, nseg, group):
    returned = [pick(y, within)]
    for shift in range(1, group):
        returned.append(
            lax.ppermute(pick(y, (within - shift) % group), "seq", group_pairs(nseg, group, group - shift))
        )
    return [((within + shift) % group, piece) for shift, piece in enumerate(returned)]


def assemble(even_parts, odd_parts, heads, shape):
    first = even_parts[0][1]
    out = jnp.zeros((heads, 2) + first.shape, first.dtype)
    zero = jnp.zeros((), jnp.int32)
    for column, parts in ((0, even_parts), (1, odd_parts)):
        for head, piece in parts:
            out = lax.dynamic_update_slice(
                out, piece[None, None], (head, jnp.int32(column), zero, zero)
            )
    return out.reshape(shape)


def body(queries, key_rows, value_rows, grad_out, partner_pos):
    heads, row_count, width = queries.shape
    blocks = row_count // BLK
    places = partner_pos.shape[2]
    group = places // blocks
    if heads != group or blocks != 2:
        raise ValueError("layout mismatch")
    nseg = lax.axis_size("seq") // group
    device = lax.axis_index("seq")
    segment = device % nseg
    within = device // nseg

    def split(x):
        return x.reshape(heads, blocks, BLK, width)

    q4, g4, k4, v4 = split(queries), split(grad_out), split(key_rows), split(value_rows)
    kv_local = gather_group(jnp.stack([k4, v4], axis=1), within, nseg, group)
    k_all = kv_local[:, 0].reshape(places, BLK, width)
    v_all = kv_local[:, 1].reshape(places, BLK, width)
    k_all, v_all, qd_odd_send = lax.optimization_barrier(
        (k_all, v_all, jnp.stack([q4[:, 1], g4[:, 1]], axis=1))
    )
    qd_odd = gather_group(qd_odd_send, within, nseg, group)
    q_odd, g_odd = qd_odd[:, 0], qd_odd[:, 1]
    q_odd, g_odd, qd_even_send = lax.optimization_barrier(
        (q_odd, g_odd, jnp.stack([q4[:, 0], g4[:, 0]], axis=1))
    )
    qd_even = gather_group(qd_even_send, within, nseg, group)
    q_even, g_even = qd_even[:, 0], qd_even[:, 1]

    odd_kv = jnp.stack([k_all[1::2], v_all[1::2]], axis=1)
    odd_send = jnp.where(segment == nseg - 1, jnp.roll(odd_kv, 1, axis=0), odd_kv)
    window_kv = lax.ppermute(odd_send, "seq", next_segment_pairs(nseg, group))

    my_partners = lax.dynamic_index_in_dim(
        lax.dynamic_index_in_dim(partner_pos, within, axis=0, keepdims=False),
        segment,
        axis=0,
        keepdims=False,
    )
    no_mask = jnp.zeros((1,), jnp.int32)
    ad_odd, own_odd, win_odd, par_odd = fused_terms(
        1, q_odd, g_odd, k_all, v_all, k_all, v_all, my_partners[1::2], no_mask
    )
    sent_odd = scatter_group(ad_odd, within, nseg, group)

    first_masked = (segment == 0).astype(jnp.int32).reshape(1)
    ad_even, own_even, win_even, par_even = fused_terms(
        0, q_even, g_even, k_all, v_all, window_kv[:, 0], window_kv[:, 1], my_partners[0::2], first_masked
    )

    ret = win_even
    ret = jnp.where(segment == 0, jnp.roll(ret, -1, axis=0), ret)
    back_pairs = [(b, a) for a, b in next_segment_pairs(nseg, group)]
    window_back = lax.ppermute(ret, "seq", back_pairs)

    place_ids = jnp.arange(places, dtype=jnp.int32)
    hits = my_partners[None, :] == place_ids[:, None]
    inverse = jnp.sum(jnp.where(hits, place_ids[None, :], 0), axis=1)
    slot = (inverse % 2) * (places // 2) + inverse // 2
    partner_terms = jnp.concatenate([par_even, par_odd], axis=0)
    partner_even = jnp.take(partner_terms, slot[0::2], axis=0)
    partner_odd = jnp.take(partner_terms, slot[1::2], axis=0)
    grads_even = (own_even + win_odd + partner_even).astype(jnp.bfloat16)
    sent_even = scatter_group(jnp.concatenate([ad_even, grads_even], axis=1), within, nseg, group)
    grads_odd = (own_odd + window_back + partner_odd).astype(jnp.bfloat16)
    sent_last = scatter_group(grads_odd, within, nseg, group)

    shape = (heads, row_count, width)

    def column(parts, index, entry=None):
        if entry is None:
            return [(h, piece[index]) for h, piece in parts]
        return [(h, piece[entry][index]) for h, piece in parts]

    return (
        assemble(column(sent_even, 0), column(sent_odd, 0), heads, shape),
        assemble(column(sent_even, 1), column(sent_odd, 1), heads, shape),
        assemble(column(sent_even, 2), column(sent_last, 0), heads, shape),
        assemble(column(sent_even, 3), column(sent_last, 1), heads, shape),
    )


def solution(mesh):
    return jax.shard_map(
        body,
        mesh=mesh,
        in_specs=(
            P("head", "seq", None),
            P("head", "seq", None),
            P("head", "seq", None),
            P("head", "seq", None),
            P("head", None, None),
        ),
        out_specs=(
            P("head", "seq", None),
            P("head", "seq", None),
            P("head", "seq", None),
            P("head", "seq", None),
        ),
        check_vma=False,
    )
```

```python
import math

import jax
import jax.numpy as jnp
from jax import lax
from jax.experimental import pallas as pl
from jax.experimental.pallas import tpu as pltpu
from jax.sharding import PartitionSpec as P

BLK = 512


def group_pairs(nseg, group, shift):
    return [
        (seg + nseg * w, seg + nseg * ((w + shift) % group))
        for seg in range(nseg)
        for w in range(group)
    ]


def next_segment_pairs(nseg, group):
    return [
        (seg + nseg * w, (seg + 1) % nseg + nseg * w)
        for seg in range(nseg)
        for w in range(group)
    ]


def block_terms(query_rows, key_block, values, grad_rows, usable):
    scaling = 1.0 / math.sqrt(query_rows.shape[-1])
    scores = (
        jnp.einsum("cid,cjd->cij", query_rows, key_block, preferred_element_type=jnp.float32)
        * scaling
    )
    scores = jnp.where(usable[:, None, :], scores, -jnp.inf)
    highest = jnp.max(scores, axis=2, keepdims=True)
    weights = jnp.exp(scores - highest)
    shares = weights / jnp.sum(weights, axis=2, keepdims=True)
    shares_low = shares.astype(jnp.bfloat16)
    attended = jnp.einsum(
        "cij,cjd->cid", shares_low, values, preferred_element_type=jnp.float32
    ).astype(jnp.bfloat16)
    attended_wide = lax.optimization_barrier(attended).astype(jnp.float32)
    row_dot = jnp.sum(grad_rows.astype(jnp.float32) * attended_wide, axis=2, keepdims=True)
    grad_probs = jnp.einsum("cid,cjd->cij", grad_rows, values, preferred_element_type=jnp.float32)
    dscore = (shares * (grad_probs - row_dot)).astype(jnp.bfloat16)
    grad_query = (
        jnp.einsum("cij,cjd->cid", dscore, key_block, preferred_element_type=jnp.float32) * scaling
    ).astype(jnp.bfloat16)
    key_terms = (
        jnp.einsum("cij,cid->cjd", dscore, query_rows, preferred_element_type=jnp.float32) * scaling
    )
    value_terms = jnp.einsum(
        "cij,cid->cjd", shares_low, grad_rows, preferred_element_type=jnp.float32
    )
    return attended, grad_query, key_terms, value_terms


def attention_kernel(index_ref, flag_ref, q_ref, g_ref, ko_ref, kw_ref, kp_ref, vo_ref, vw_ref, vp_ref, *rest):
    ad_ref, own_ref, win_ref, par_ref = rest[-4:]
    place = pl.program_id(0)
    q = q_ref[0]
    g = g_ref[0]
    keys = (ko_ref[0], kw_ref[0], kp_ref[0])
    values = (vo_ref[0], vw_ref[0], vp_ref[0])
    scaling = 1.0 / math.sqrt(q.shape[-1])
    rows_by_rows = (((1,), (1,)), ((), ()))
    cols_by_cols = (((0,), (0,)), ((), ()))
    scores = [
        lax.dot_general(q, k, rows_by_rows, preferred_element_type=jnp.float32) * scaling
        for k in keys
    ]
    kill = jnp.where(place == 0, flag_ref[0], 0)
    scores[1] = jnp.where(kill > 0, -jnp.inf, scores[1])
    highest = jnp.maximum(
        jnp.maximum(jnp.max(scores[0], axis=1, keepdims=True), jnp.max(scores[1], axis=1, keepdims=True)),
        jnp.max(scores[2], axis=1, keepdims=True),
    )
    weights = [jnp.exp(s - highest) for s in scores]
    total = (
        jnp.sum(weights[0], axis=1, keepdims=True)
        + jnp.sum(weights[1], axis=1, keepdims=True)
        + jnp.sum(weights[2], axis=1, keepdims=True)
    )
    shares = [w / total for w in weights]
    shares_low = [s.astype(jnp.bfloat16) for s in shares]
    attended_wide = jnp.dot(shares_low[0], values[0], preferred_element_type=jnp.float32)
    attended_wide = attended_wide + jnp.dot(shares_low[1], values[1], preferred_element_type=jnp.float32)
    attended_wide = attended_wide + jnp.dot(shares_low[2], values[2], preferred_element_type=jnp.float32)
    attended = attended_wide.astype(jnp.bfloat16)
    ad_ref[0, 0] = attended
    row_dot = jnp.sum(g.astype(jnp.float32) * attended.astype(jnp.float32), axis=1, keepdims=True)
    dq = None
    for part in range(3):
        grad_probs = lax.dot_general(g, values[part], rows_by_rows, preferred_element_type=jnp.float32)
        dscore = (shares[part] * (grad_probs - row_dot)).astype(jnp.bfloat16)
        term = jnp.dot(dscore, keys[part], preferred_element_type=jnp.float32)
        dq = term if dq is None else dq + term
        out_ref = (own_ref.at[0], win_ref.at[0], par_ref.at[0, 0])[part]
        out_ref[0] = (
            lax.dot_general(dscore, q, cols_by_cols, preferred_element_type=jnp.float32) * scaling
        )
        out_ref[1] = lax.dot_general(
            shares_low[part], g, cols_by_cols, preferred_element_type=jnp.float32
        )
    ad_ref[0, 1] = (dq * scaling).astype(jnp.bfloat16)


def fused_terms(parity, q_rows, g_rows, k_all, v_all, k_window, v_window, partner_index, first_masked, partner_buffer=None):
    places, rows, width = q_rows.shape
    row_spec = pl.BlockSpec((1, rows, width), lambda p, idx, flag: (p, 0, 0))
    own_spec = pl.BlockSpec((1, rows, width), lambda p, idx, flag: (2 * p + parity, 0, 0))
    partner_spec = pl.BlockSpec((1, rows, width), lambda p, idx, flag: (idx[p], 0, 0))
    if parity:
        window_spec = pl.BlockSpec((1, rows, width), lambda p, idx, flag: (2 * p, 0, 0))
    else:
        window_spec = row_spec
    pair_spec = pl.BlockSpec((1, 2, rows, width), lambda p, idx, flag: (p, 0, 0, 0))
    target_spec = pl.BlockSpec(
        (1, 1, 2, rows, width), lambda p, idx, flag: (idx[p] % 2, idx[p] // 2, 0, 0, 0)
    )
    in_specs = [row_spec, row_spec, own_spec, window_spec, partner_spec, own_spec, window_spec, partner_spec]
    operands = [partner_index, first_masked, q_rows, g_rows, k_all, k_window, k_all, v_all, v_window, v_all]
    aliases = {}
    if partner_buffer is not None:
        in_specs.append(pl.BlockSpec(memory_space=pl.ANY))
        aliases = {len(operands): 3}
        operands.append(partner_buffer)
    flops = 36 * places * rows * rows * width
    return pl.pallas_call(
        attention_kernel,
        grid_spec=pltpu.PrefetchScalarGridSpec(
            num_scalar_prefetch=2,
            grid=(places,),
            in_specs=in_specs,
            out_specs=[pair_spec, pair_spec, pair_spec, target_spec],
        ),
        out_shape=[jax.ShapeDtypeStruct((places, 2, rows, width), jnp.bfloat16)]
        + [jax.ShapeDtypeStruct((places, 2, rows, width), jnp.float32)] * 2
        + [jax.ShapeDtypeStruct((2, places, 2, rows, width), jnp.float32)],
        input_output_aliases=aliases,
        cost_estimate=pl.CostEstimate(
            flops=flops,
            transcendentals=3 * places * rows * rows,
            bytes_accessed=places * rows * width * 60,
        ),
    )(*operands)


def interleave(even, odd):
    return jnp.stack([even, odd], axis=1).reshape((-1,) + even.shape[1:])


def pick(tree, index):
    return jax.tree.map(lambda x: lax.dynamic_index_in_dim(x, index, axis=0, keepdims=False), tree)


def gather_group(x, within, nseg, group):
    received = [pick(x, within)]
    for shift in range(1, group):
        received.append(lax.ppermute(pick(x, (within + shift) % group), "seq", group_pairs(nseg, group, shift)))

    def place(*pieces):
        out = jnp.zeros((group,) + pieces[0].shape, pieces[0].dtype)
        for shift, piece in enumerate(pieces):
            out = lax.dynamic_update_index_in_dim(out, piece, (within - shift) % group, 0)
        return out

    return jax.tree.map(place, *received)


def scatter_group(y, within, nseg, group):
    returned = [pick(y, within)]
    for shift in range(1, group):
        returned.append(
            lax.ppermute(pick(y, (within - shift) % group), "seq", group_pairs(nseg, group, group - shift))
        )
    return [((within + shift) % group, piece) for shift, piece in enumerate(returned)]


def assemble(even_parts, odd_parts, heads, shape):
    first = even_parts[0][1]
    out = jnp.zeros((heads, 2) + first.shape, first.dtype)
    zero = jnp.zeros((), jnp.int32)
    for column, parts in ((0, even_parts), (1, odd_parts)):
        for head, piece in parts:
            out = lax.dynamic_update_slice(
                out, piece[None, None], (head, jnp.int32(column), zero, zero)
            )
    return out.reshape(shape)


def body(queries, key_rows, value_rows, grad_out, partner_pos):
    heads, row_count, width = queries.shape
    blocks = row_count // BLK
    places = partner_pos.shape[2]
    group = places // blocks
    if heads != group or blocks != 2:
        raise ValueError("layout mismatch")
    nseg = lax.axis_size("seq") // group
    device = lax.axis_index("seq")
    segment = device % nseg
    within = device // nseg

    def split(x):
        return x.reshape(heads, blocks, BLK, width)

    q4, g4, k4, v4 = split(queries), split(grad_out), split(key_rows), split(value_rows)
    kv_local = gather_group(jnp.stack([k4, v4], axis=1), within, nseg, group)
    k_all = kv_local[:, 0].reshape(places, BLK, width)
    v_all = kv_local[:, 1].reshape(places, BLK, width)
    k_all, v_all, qd_odd_send = lax.optimization_barrier(
        (k_all, v_all, jnp.stack([q4[:, 1], g4[:, 1]], axis=1))
    )
    qd_odd = gather_group(qd_odd_send, within, nseg, group)
    q_odd, g_odd = qd_odd[:, 0], qd_odd[:, 1]
    q_odd, g_odd, qd_even_send = lax.optimization_barrier(
        (q_odd, g_odd, jnp.stack([q4[:, 0], g4[:, 0]], axis=1))
    )
    qd_even = gather_group(qd_even_send, within, nseg, group)
    q_even, g_even = qd_even[:, 0], qd_even[:, 1]

    odd_kv = jnp.stack([k_all[1::2], v_all[1::2]], axis=1)
    odd_send = jnp.where(segment == nseg - 1, jnp.roll(odd_kv, 1, axis=0), odd_kv)
    window_kv = lax.ppermute(odd_send, "seq", next_segment_pairs(nseg, group))

    my_partners = lax.dynamic_index_in_dim(
        lax.dynamic_index_in_dim(partner_pos, within, axis=0, keepdims=False),
        segment,
        axis=0,
        keepdims=False,
    )
    no_mask = jnp.zeros((1,), jnp.int32)
    ad_odd, own_odd, win_odd, par_odd = fused_terms(
        1, q_odd, g_odd, k_all, v_all, k_all, v_all, my_partners[1::2], no_mask
    )
    sent_odd = scatter_group(ad_odd, within, nseg, group)

    first_masked = (segment == 0).astype(jnp.int32).reshape(1)
    ad_even, own_even, win_even, par_all = fused_terms(
        0, q_even, g_even, k_all, v_all, window_kv[:, 0], window_kv[:, 1], my_partners[0::2], first_masked, par_odd
    )

    ret = win_even
    ret = jnp.where(segment == 0, jnp.roll(ret, -1, axis=0), ret)
    back_pairs = [(b, a) for a, b in next_segment_pairs(nseg, group)]
    window_back = lax.ppermute(ret, "seq", back_pairs)

    partner_even = par_all[0]
    partner_odd = par_all[1]
    grads_even = (own_even + win_odd + partner_even).astype(jnp.bfloat16)
    sent_even = scatter_group(jnp.concatenate([ad_even, grads_even], axis=1), within, nseg, group)
    grads_odd = (own_odd + window_back + partner_odd).astype(jnp.bfloat16)
    sent_last = scatter_group(grads_odd, within, nseg, group)

    shape = (heads, row_count, width)

    def column(parts, index, entry=None):
        if entry is None:
            return [(h, piece[index]) for h, piece in parts]
        return [(h, piece[entry][index]) for h, piece in parts]

    return (
        assemble(column(sent_even, 0), column(sent_odd, 0), heads, shape),
        assemble(column(sent_even, 1), column(sent_odd, 1), heads, shape),
        assemble(column(sent_even, 2), column(sent_last, 0), heads, shape),
        assemble(column(sent_even, 3), column(sent_last, 1), heads, shape),
    )


def solution(mesh):
    return jax.shard_map(
        body,
        mesh=mesh,
        in_specs=(
            P("head", "seq", None),
            P("head", "seq", None),
            P("head", "seq", None),
            P("head", "seq", None),
            P("head", None, None),
        ),
        out_specs=(
            P("head", "seq", None),
            P("head", "seq", None),
            P("head", "seq", None),
            P("head", "seq", None),
        ),
        check_vma=False,
    )
```

```python
import math

import jax
import jax.numpy as jnp
from jax import lax
from jax.experimental import pallas as pl
from jax.experimental.pallas import tpu as pltpu
from jax.sharding import PartitionSpec as P

BLK = 512


def group_pairs(nseg, group, shift):
    return [
        (seg + nseg * w, seg + nseg * ((w + shift) % group))
        for seg in range(nseg)
        for w in range(group)
    ]


def next_segment_pairs(nseg, group):
    return [
        (seg + nseg * w, (seg + 1) % nseg + nseg * w)
        for seg in range(nseg)
        for w in range(group)
    ]


def block_terms(query_rows, key_block, values, grad_rows, usable):
    scaling = 1.0 / math.sqrt(query_rows.shape[-1])
    scores = (
        jnp.einsum("cid,cjd->cij", query_rows, key_block, preferred_element_type=jnp.float32)
        * scaling
    )
    scores = jnp.where(usable[:, None, :], scores, -jnp.inf)
    highest = jnp.max(scores, axis=2, keepdims=True)
    weights = jnp.exp(scores - highest)
    shares = weights / jnp.sum(weights, axis=2, keepdims=True)
    shares_low = shares.astype(jnp.bfloat16)
    attended = jnp.einsum(
        "cij,cjd->cid", shares_low, values, preferred_element_type=jnp.float32
    ).astype(jnp.bfloat16)
    attended_wide = lax.optimization_barrier(attended).astype(jnp.float32)
    row_dot = jnp.sum(grad_rows.astype(jnp.float32) * attended_wide, axis=2, keepdims=True)
    grad_probs = jnp.einsum("cid,cjd->cij", grad_rows, values, preferred_element_type=jnp.float32)
    dscore = (shares * (grad_probs - row_dot)).astype(jnp.bfloat16)
    grad_query = (
        jnp.einsum("cij,cjd->cid", dscore, key_block, preferred_element_type=jnp.float32) * scaling
    ).astype(jnp.bfloat16)
    key_terms = (
        jnp.einsum("cij,cid->cjd", dscore, query_rows, preferred_element_type=jnp.float32) * scaling
    )
    value_terms = jnp.einsum(
        "cij,cid->cjd", shares_low, grad_rows, preferred_element_type=jnp.float32
    )
    return attended, grad_query, key_terms, value_terms


def attention_kernel(index_ref, flag_ref, q_ref, g_ref, ko_ref, kw_ref, kp_ref, vo_ref, vw_ref, vp_ref, *rest):
    ad_ref, own_ref, win_ref, par_ref = rest[-4:]
    place = pl.program_id(0)
    q = q_ref[0]
    g = g_ref[0]
    keys = (ko_ref[0], kw_ref[0], kp_ref[0])
    values = (vo_ref[0], vw_ref[0], vp_ref[0])
    scaling = 1.0 / math.sqrt(q.shape[-1])
    rows_by_rows = (((1,), (1,)), ((), ()))
    cols_by_cols = (((0,), (0,)), ((), ()))
    scores = [
        lax.dot_general(q, k, rows_by_rows, preferred_element_type=jnp.float32) * scaling
        for k in keys
    ]
    kill = jnp.where(place == 0, flag_ref[0], 0)
    scores[1] = jnp.where(kill > 0, -jnp.inf, scores[1])
    highest = jnp.maximum(
        jnp.maximum(jnp.max(scores[0], axis=1, keepdims=True), jnp.max(scores[1], axis=1, keepdims=True)),
        jnp.max(scores[2], axis=1, keepdims=True),
    )
    weights = [jnp.exp(s - highest) for s in scores]
    total = (
        jnp.sum(weights[0], axis=1, keepdims=True)
        + jnp.sum(weights[1], axis=1, keepdims=True)
        + jnp.sum(weights[2], axis=1, keepdims=True)
    )
    shares = [w / total for w in weights]
    shares_low = [s.astype(jnp.bfloat16) for s in shares]
    attended_wide = jnp.dot(shares_low[0], values[0], preferred_element_type=jnp.float32)
    attended_wide = attended_wide + jnp.dot(shares_low[1], values[1], preferred_element_type=jnp.float32)
    attended_wide = attended_wide + jnp.dot(shares_low[2], values[2], preferred_element_type=jnp.float32)
    attended = attended_wide.astype(jnp.bfloat16)
    ad_ref[0, 0] = attended
    row_dot = jnp.sum(g.astype(jnp.float32) * attended.astype(jnp.float32), axis=1, keepdims=True)
    dq = None
    for part in range(3):
        grad_probs = lax.dot_general(g, values[part], rows_by_rows, preferred_element_type=jnp.float32)
        dscore = (shares[part] * (grad_probs - row_dot)).astype(jnp.bfloat16)
        term = jnp.dot(dscore, keys[part], preferred_element_type=jnp.float32)
        dq = term if dq is None else dq + term
        out_ref = (own_ref.at[0], win_ref.at[0], par_ref.at[0, 0])[part]
        out_ref[0] = (
            lax.dot_general(dscore, q, cols_by_cols, preferred_element_type=jnp.float32) * scaling
        )
        out_ref[1] = lax.dot_general(
            shares_low[part], g, cols_by_cols, preferred_element_type=jnp.float32
        )
    ad_ref[0, 1] = (dq * scaling).astype(jnp.bfloat16)


def fused_terms(parity, q_rows, g_rows, k_all, v_all, k_window, v_window, partner_index, first_masked, partner_buffer=None):
    places, rows, width = q_rows.shape
    row_spec = pl.BlockSpec((1, rows, width), lambda p, idx, flag: (p, 0, 0))
    own_spec = pl.BlockSpec((1, rows, width), lambda p, idx, flag: (2 * p + parity, 0, 0))
    partner_spec = pl.BlockSpec((1, rows, width), lambda p, idx, flag: (idx[p], 0, 0))
    if parity:
        window_spec = pl.BlockSpec((1, rows, width), lambda p, idx, flag: (2 * p, 0, 0))
    else:
        window_spec = row_spec
    pair_spec = pl.BlockSpec((1, 2, rows, width), lambda p, idx, flag: (p, 0, 0, 0))
    target_spec = pl.BlockSpec(
        (1, 1, 2, rows, width), lambda p, idx, flag: (idx[p] % 2, idx[p] // 2, 0, 0, 0)
    )
    in_specs = [row_spec, row_spec, own_spec, window_spec, partner_spec, own_spec, window_spec, partner_spec]
    operands = [partner_index, first_masked, q_rows, g_rows, k_all, k_window, k_all, v_all, v_window, v_all]
    aliases = {}
    if partner_buffer is not None:
        in_specs.append(pl.BlockSpec(memory_space=pl.ANY))
        aliases = {len(operands): 3}
        operands.append(partner_buffer)
    flops = 36 * places * rows * rows * width
    return pl.pallas_call(
        attention_kernel,
        grid_spec=pltpu.PrefetchScalarGridSpec(
            num_scalar_prefetch=2,
            grid=(places,),
            in_specs=in_specs,
            out_specs=[pair_spec, pair_spec, pair_spec, target_spec],
        ),
        out_shape=[jax.ShapeDtypeStruct((places, 2, rows, width), jnp.bfloat16)]
        + [jax.ShapeDtypeStruct((places, 2, rows, width), jnp.float32)] * 2
        + [jax.ShapeDtypeStruct((2, places, 2, rows, width), jnp.float32)],
        input_output_aliases=aliases,
        cost_estimate=pl.CostEstimate(
            flops=flops,
            transcendentals=3 * places * rows * rows,
            bytes_accessed=places * rows * width * 60,
        ),
    )(*operands)


def interleave(even, odd):
    return jnp.stack([even, odd], axis=1).reshape((-1,) + even.shape[1:])


def pick(tree, index):
    return jax.tree.map(lambda x: lax.dynamic_index_in_dim(x, index, axis=0, keepdims=False), tree)


def gather_group(x, within, nseg, group):
    received = [pick(x, within)]
    for shift in range(1, group):
        received.append(lax.ppermute(pick(x, (within + shift) % group), "seq", group_pairs(nseg, group, shift)))

    def place(*pieces):
        out = jnp.zeros((group,) + pieces[0].shape, pieces[0].dtype)
        for shift, piece in enumerate(pieces):
            out = lax.dynamic_update_index_in_dim(out, piece, (within - shift) % group, 0)
        return out

    return jax.tree.map(place, *received)


def scatter_group(y, within, nseg, group):
    returned = [pick(y, within)]
    for shift in range(1, group):
        returned.append(
            lax.ppermute(pick(y, (within - shift) % group), "seq", group_pairs(nseg, group, group - shift))
        )
    return [((within + shift) % group, piece) for shift, piece in enumerate(returned)]


def assemble(even_parts, odd_parts, heads, shape):
    first = even_parts[0][1]
    out = jnp.zeros((heads, 2) + first.shape, first.dtype)
    zero = jnp.zeros((), jnp.int32)
    for column, parts in ((0, even_parts), (1, odd_parts)):
        for head, piece in parts:
            out = lax.dynamic_update_slice(
                out, piece[None, None], (head, jnp.int32(column), zero, zero)
            )
    return out.reshape(shape)


def body(queries, key_rows, value_rows, grad_out, partner_pos):
    heads, row_count, width = queries.shape
    blocks = row_count // BLK
    places = partner_pos.shape[2]
    group = places // blocks
    if heads != group or blocks != 2:
        raise ValueError("layout mismatch")
    nseg = lax.axis_size("seq") // group
    device = lax.axis_index("seq")
    segment = device % nseg
    within = device // nseg

    def split(x):
        return x.reshape(heads, blocks, BLK, width)

    q4, g4, k4, v4 = split(queries), split(grad_out), split(key_rows), split(value_rows)
    kv_local = gather_group(jnp.stack([k4, v4], axis=1), within, nseg, group)
    k_all = kv_local[:, 0].reshape(places, BLK, width)
    v_all = kv_local[:, 1].reshape(places, BLK, width)
    k_all, v_all, qd_odd_send = lax.optimization_barrier(
        (k_all, v_all, jnp.stack([q4[:, 1], g4[:, 1]], axis=1))
    )
    qd_odd = gather_group(qd_odd_send, within, nseg, group)
    q_odd, g_odd = qd_odd[:, 0], qd_odd[:, 1]
    q_odd, g_odd, qd_even_send = lax.optimization_barrier(
        (q_odd, g_odd, jnp.stack([q4[:, 0], g4[:, 0]], axis=1))
    )
    qd_even = gather_group(qd_even_send, within, nseg, group)
    q_even, g_even = qd_even[:, 0], qd_even[:, 1]

    odd_kv = jnp.stack([k_all[1::2], v_all[1::2]], axis=1)
    odd_send = jnp.where(segment == nseg - 1, jnp.roll(odd_kv, 1, axis=0), odd_kv)
    window_kv = lax.ppermute(odd_send, "seq", next_segment_pairs(nseg, group))

    my_partners = lax.dynamic_index_in_dim(
        lax.dynamic_index_in_dim(partner_pos, within, axis=0, keepdims=False),
        segment,
        axis=0,
        keepdims=False,
    )
    no_mask = jnp.zeros((1,), jnp.int32)
    ad_odd, own_odd, win_odd, par_odd = fused_terms(
        1, q_odd, g_odd, k_all, v_all, k_all, v_all, my_partners[1::2], no_mask
    )
    sent_odd = scatter_group(ad_odd, within, nseg, group)

    first_masked = (segment == 0).astype(jnp.int32).reshape(1)
    ad_even, own_even, win_even, par_all = fused_terms(
        0, q_even, g_even, k_all, v_all, window_kv[:, 0], window_kv[:, 1], my_partners[0::2], first_masked, par_odd
    )

    ret = win_even
    ret = jnp.where(segment == 0, jnp.roll(ret, -1, axis=0), ret)
    back_pairs = [(b, a) for a, b in next_segment_pairs(nseg, group)]
    window_back = lax.ppermute(ret, "seq", back_pairs)

    partner_even = par_all[0]
    partner_odd = par_all[1]
    grads_even = (own_even + win_odd + partner_even).astype(jnp.bfloat16)
    sent_even = scatter_group(jnp.concatenate([ad_even, grads_even], axis=1), within, nseg, group)
    grads_even, own_odd, partner_odd = lax.optimization_barrier((grads_even, own_odd, partner_odd))
    grads_odd = (own_odd + window_back + partner_odd).astype(jnp.bfloat16)
    sent_last = scatter_group(grads_odd, within, nseg, group)

    shape = (heads, row_count, width)

    def column(parts, index, entry=None):
        if entry is None:
            return [(h, piece[index]) for h, piece in parts]
        return [(h, piece[entry][index]) for h, piece in parts]

    return (
        assemble(column(sent_even, 0), column(sent_odd, 0), heads, shape),
        assemble(column(sent_even, 1), column(sent_odd, 1), heads, shape),
        assemble(column(sent_even, 2), column(sent_last, 0), heads, shape),
        assemble(column(sent_even, 3), column(sent_last, 1), heads, shape),
    )


def solution(mesh):
    return jax.shard_map(
        body,
        mesh=mesh,
        in_specs=(
            P("head", "seq", None),
            P("head", "seq", None),
            P("head", "seq", None),
            P("head", "seq", None),
            P("head", None, None),
        ),
        out_specs=(
            P("head", "seq", None),
            P("head", "seq", None),
            P("head", "seq", None),
            P("head", "seq", None),
        ),
        check_vma=False,
    )
```

```python
import math

import jax
import jax.numpy as jnp
from jax import lax
from jax.experimental import pallas as pl
from jax.experimental.pallas import tpu as pltpu
from jax.sharding import PartitionSpec as P

BLK = 512


def group_pairs(nseg, group, shift):
    return [
        (seg + nseg * w, seg + nseg * ((w + shift) % group))
        for seg in range(nseg)
        for w in range(group)
    ]


def next_segment_pairs(nseg, group):
    return [
        (seg + nseg * w, (seg + 1) % nseg + nseg * w)
        for seg in range(nseg)
        for w in range(group)
    ]


def block_terms(query_rows, key_block, values, grad_rows, usable):
    scaling = 1.0 / math.sqrt(query_rows.shape[-1])
    scores = (
        jnp.einsum("cid,cjd->cij", query_rows, key_block, preferred_element_type=jnp.float32)
        * scaling
    )
    scores = jnp.where(usable[:, None, :], scores, -jnp.inf)
    highest = jnp.max(scores, axis=2, keepdims=True)
    weights = jnp.exp(scores - highest)
    shares = weights / jnp.sum(weights, axis=2, keepdims=True)
    shares_low = shares.astype(jnp.bfloat16)
    attended = jnp.einsum(
        "cij,cjd->cid", shares_low, values, preferred_element_type=jnp.float32
    ).astype(jnp.bfloat16)
    attended_wide = lax.optimization_barrier(attended).astype(jnp.float32)
    row_dot = jnp.sum(grad_rows.astype(jnp.float32) * attended_wide, axis=2, keepdims=True)
    grad_probs = jnp.einsum("cid,cjd->cij", grad_rows, values, preferred_element_type=jnp.float32)
    dscore = (shares * (grad_probs - row_dot)).astype(jnp.bfloat16)
    grad_query = (
        jnp.einsum("cij,cjd->cid", dscore, key_block, preferred_element_type=jnp.float32) * scaling
    ).astype(jnp.bfloat16)
    key_terms = (
        jnp.einsum("cij,cid->cjd", dscore, query_rows, preferred_element_type=jnp.float32) * scaling
    )
    value_terms = jnp.einsum(
        "cij,cid->cjd", shares_low, grad_rows, preferred_element_type=jnp.float32
    )
    return attended, grad_query, key_terms, value_terms


def attention_kernel(index_ref, flag_ref, q_ref, g_ref, ko_ref, kw_ref, kp_ref, vo_ref, vw_ref, vp_ref, *rest):
    ad_ref, own_ref, win_ref, par_ref = rest[-4:]
    place = pl.program_id(0)
    q = q_ref[0]
    g = g_ref[0]
    keys = (ko_ref[0], kw_ref[0], kp_ref[0])
    values = (vo_ref[0], vw_ref[0], vp_ref[0])
    scaling = 1.0 / math.sqrt(q.shape[-1])
    rows_by_rows = (((1,), (1,)), ((), ()))
    cols_by_cols = (((0,), (0,)), ((), ()))
    scores = [
        lax.dot_general(q, k, rows_by_rows, preferred_element_type=jnp.float32) * scaling
        for k in keys
    ]
    kill = jnp.where(place == 0, flag_ref[0], 0)
    scores[1] = jnp.where(kill > 0, -jnp.inf, scores[1])
    highest = jnp.maximum(
        jnp.maximum(jnp.max(scores[0], axis=1, keepdims=True), jnp.max(scores[1], axis=1, keepdims=True)),
        jnp.max(scores[2], axis=1, keepdims=True),
    )
    weights = [jnp.exp(s - highest) for s in scores]
    total = (
        jnp.sum(weights[0], axis=1, keepdims=True)
        + jnp.sum(weights[1], axis=1, keepdims=True)
        + jnp.sum(weights[2], axis=1, keepdims=True)
    )
    shares = [w / total for w in weights]
    shares_low = [s.astype(jnp.bfloat16) for s in shares]
    attended_wide = jnp.dot(shares_low[0], values[0], preferred_element_type=jnp.float32)
    attended_wide = attended_wide + jnp.dot(shares_low[1], values[1], preferred_element_type=jnp.float32)
    attended_wide = attended_wide + jnp.dot(shares_low[2], values[2], preferred_element_type=jnp.float32)
    attended = attended_wide.astype(jnp.bfloat16)
    ad_ref[0, 0] = attended
    row_dot = jnp.sum(g.astype(jnp.float32) * attended.astype(jnp.float32), axis=1, keepdims=True)
    dq = None
    for part in range(3):
        grad_probs = lax.dot_general(g, values[part], rows_by_rows, preferred_element_type=jnp.float32)
        dscore = (shares[part] * (grad_probs - row_dot)).astype(jnp.bfloat16)
        term = jnp.dot(dscore, keys[part], preferred_element_type=jnp.float32)
        dq = term if dq is None else dq + term
        out_ref = (own_ref.at[0], win_ref.at[0], par_ref.at[0, 0])[part]
        out_ref[0] = (
            lax.dot_general(dscore, q, cols_by_cols, preferred_element_type=jnp.float32) * scaling
        )
        out_ref[1] = lax.dot_general(
            shares_low[part], g, cols_by_cols, preferred_element_type=jnp.float32
        )
    ad_ref[0, 1] = (dq * scaling).astype(jnp.bfloat16)


def fused_terms(parity, q_rows, g_rows, k_all, v_all, k_window, v_window, partner_index, first_masked, partner_buffer=None):
    places, rows, width = q_rows.shape
    row_spec = pl.BlockSpec((1, rows, width), lambda p, idx, flag: (p, 0, 0))
    own_spec = pl.BlockSpec((1, rows, width), lambda p, idx, flag: (2 * p + parity, 0, 0))
    partner_spec = pl.BlockSpec((1, rows, width), lambda p, idx, flag: (idx[p], 0, 0))
    if parity:
        window_spec = pl.BlockSpec((1, rows, width), lambda p, idx, flag: (2 * p, 0, 0))
    else:
        window_spec = row_spec
    pair_spec = pl.BlockSpec((1, 2, rows, width), lambda p, idx, flag: (p, 0, 0, 0))
    target_spec = pl.BlockSpec(
        (1, 1, 2, rows, width), lambda p, idx, flag: (idx[p] % 2, idx[p] // 2, 0, 0, 0)
    )
    in_specs = [row_spec, row_spec, own_spec, window_spec, partner_spec, own_spec, window_spec, partner_spec]
    operands = [partner_index, first_masked, q_rows, g_rows, k_all, k_window, k_all, v_all, v_window, v_all]
    aliases = {}
    if partner_buffer is not None:
        in_specs.append(pl.BlockSpec(memory_space=pl.ANY))
        aliases = {len(operands): 3}
        operands.append(partner_buffer)
    flops = 36 * places * rows * rows * width
    return pl.pallas_call(
        attention_kernel,
        grid_spec=pltpu.PrefetchScalarGridSpec(
            num_scalar_prefetch=2,
            grid=(places,),
            in_specs=in_specs,
            out_specs=[pair_spec, pair_spec, pair_spec, target_spec],
        ),
        out_shape=[jax.ShapeDtypeStruct((places, 2, rows, width), jnp.bfloat16)]
        + [jax.ShapeDtypeStruct((places, 2, rows, width), jnp.float32)] * 2
        + [jax.ShapeDtypeStruct((2, places, 2, rows, width), jnp.float32)],
        input_output_aliases=aliases,
        cost_estimate=pl.CostEstimate(
            flops=flops,
            transcendentals=3 * places * rows * rows,
            bytes_accessed=places * rows * width * 60,
        ),
    )(*operands)


def interleave(even, odd):
    return jnp.stack([even, odd], axis=1).reshape((-1,) + even.shape[1:])


def pick(tree, index):
    return jax.tree.map(lambda x: lax.dynamic_index_in_dim(x, index, axis=0, keepdims=False), tree)


def gather_group(x, within, nseg, group):
    received = [pick(x, within)]
    for shift in range(1, group):
        received.append(lax.ppermute(pick(x, (within + shift) % group), "seq", group_pairs(nseg, group, shift)))

    def place(*pieces):
        out = jnp.zeros((group,) + pieces[0].shape, pieces[0].dtype)
        for shift, piece in enumerate(pieces):
            out = lax.dynamic_update_index_in_dim(out, piece, (within - shift) % group, 0)
        return out

    return jax.tree.map(place, *received)


def scatter_group(y, within, nseg, group):
    returned = [pick(y, within)]
    for shift in range(1, group):
        returned.append(
            lax.ppermute(pick(y, (within - shift) % group), "seq", group_pairs(nseg, group, group - shift))
        )
    return [((within + shift) % group, piece) for shift, piece in enumerate(returned)]


def assemble(even_parts, odd_parts, heads, shape):
    first = even_parts[0][1]
    out = jnp.zeros((heads, 2) + first.shape, first.dtype)
    zero = jnp.zeros((), jnp.int32)
    for column, parts in ((0, even_parts), (1, odd_parts)):
        for head, piece in parts:
            out = lax.dynamic_update_slice(
                out, piece[None, None], (head, jnp.int32(column), zero, zero)
            )
    return out.reshape(shape)


def body(queries, key_rows, value_rows, grad_out, partner_pos):
    heads, row_count, width = queries.shape
    blocks = row_count // BLK
    places = partner_pos.shape[2]
    group = places // blocks
    if heads != group or blocks != 2:
        raise ValueError("layout mismatch")
    nseg = lax.axis_size("seq") // group
    device = lax.axis_index("seq")
    segment = device % nseg
    within = device // nseg

    def split(x):
        return x.reshape(heads, blocks, BLK, width)

    q4, g4, k4, v4 = split(queries), split(grad_out), split(key_rows), split(value_rows)
    kv_local = gather_group(jnp.stack([k4, v4], axis=1), within, nseg, group)
    k_all = kv_local[:, 0].reshape(places, BLK, width)
    v_all = kv_local[:, 1].reshape(places, BLK, width)
    k_all, v_all, qd_even_send = lax.optimization_barrier(
        (k_all, v_all, jnp.stack([q4[:, 0], g4[:, 0]], axis=1))
    )
    qd_even = gather_group(qd_even_send, within, nseg, group)
    q_even, g_even = qd_even[:, 0], qd_even[:, 1]
    q_even, g_even, qd_odd_send = lax.optimization_barrier(
        (q_even, g_even, jnp.stack([q4[:, 1], g4[:, 1]], axis=1))
    )
    qd_odd = gather_group(qd_odd_send, within, nseg, group)
    q_odd, g_odd = qd_odd[:, 0], qd_odd[:, 1]

    odd_kv = jnp.stack([k_all[1::2], v_all[1::2]], axis=1)
    odd_send = jnp.where(segment == nseg - 1, jnp.roll(odd_kv, 1, axis=0), odd_kv)
    window_kv = lax.ppermute(odd_send, "seq", next_segment_pairs(nseg, group))

    my_partners = lax.dynamic_index_in_dim(
        lax.dynamic_index_in_dim(partner_pos, within, axis=0, keepdims=False),
        segment,
        axis=0,
        keepdims=False,
    )
    first_masked = (segment == 0).astype(jnp.int32).reshape(1)
    ad_even, own_even, win_even, par_even = fused_terms(
        0, q_even, g_even, k_all, v_all, window_kv[:, 0], window_kv[:, 1], my_partners[0::2], first_masked
    )
    sent_even = scatter_group(ad_even, within, nseg, group)

    ret = win_even
    ret = jnp.where(segment == 0, jnp.roll(ret, -1, axis=0), ret)
    back_pairs = [(b, a) for a, b in next_segment_pairs(nseg, group)]
    window_back = lax.ppermute(ret, "seq", back_pairs)

    no_mask = jnp.zeros((1,), jnp.int32)
    ad_odd, own_odd, win_odd, par_all = fused_terms(
        1, q_odd, g_odd, k_all, v_all, k_all, v_all, my_partners[1::2], no_mask, par_even
    )
    grads_even = (own_even + win_odd + par_all[0]).astype(jnp.bfloat16)
    grads_odd = (own_odd + window_back + par_all[1]).astype(jnp.bfloat16)
    sent_rest = scatter_group(jnp.concatenate([ad_odd, grads_even, grads_odd], axis=1), within, nseg, group)

    shape = (heads, row_count, width)

    def column(parts, index, entry=None):
        if entry is None:
            return [(h, piece[index]) for h, piece in parts]
        return [(h, piece[entry][index]) for h, piece in parts]

    return (
        assemble(column(sent_even, 0), column(sent_rest, 0), heads, shape),
        assemble(column(sent_even, 1), column(sent_rest, 1), heads, shape),
        assemble(column(sent_rest, 2), column(sent_rest, 4), heads, shape),
        assemble(column(sent_rest, 3), column(sent_rest, 5), heads, shape),
    )


def solution(mesh):
    return jax.shard_map(
        body,
        mesh=mesh,
        in_specs=(
            P("head", "seq", None),
            P("head", "seq", None),
            P("head", "seq", None),
            P("head", "seq", None),
            P("head", None, None),
        ),
        out_specs=(
            P("head", "seq", None),
            P("head", "seq", None),
            P("head", "seq", None),
            P("head", "seq", None),
        ),
        check_vma=False,
    )
```

```python
import math

import jax
import jax.numpy as jnp
from jax import lax
from jax.experimental import pallas as pl
from jax.experimental.pallas import tpu as pltpu
from jax.sharding import PartitionSpec as P

BLK = 512


def group_pairs(nseg, group, shift):
    return [
        (seg + nseg * w, seg + nseg * ((w + shift) % group))
        for seg in range(nseg)
        for w in range(group)
    ]


def next_segment_pairs(nseg, group):
    return [
        (seg + nseg * w, (seg + 1) % nseg + nseg * w)
        for seg in range(nseg)
        for w in range(group)
    ]


def block_terms(query_rows, key_block, values, grad_rows, usable):
    scaling = 1.0 / math.sqrt(query_rows.shape[-1])
    scores = (
        jnp.einsum("cid,cjd->cij", query_rows, key_block, preferred_element_type=jnp.float32)
        * scaling
    )
    scores = jnp.where(usable[:, None, :], scores, -jnp.inf)
    highest = jnp.max(scores, axis=2, keepdims=True)
    weights = jnp.exp(scores - highest)
    shares = weights / jnp.sum(weights, axis=2, keepdims=True)
    shares_low = shares.astype(jnp.bfloat16)
    attended = jnp.einsum(
        "cij,cjd->cid", shares_low, values, preferred_element_type=jnp.float32
    ).astype(jnp.bfloat16)
    attended_wide = lax.optimization_barrier(attended).astype(jnp.float32)
    row_dot = jnp.sum(grad_rows.astype(jnp.float32) * attended_wide, axis=2, keepdims=True)
    grad_probs = jnp.einsum("cid,cjd->cij", grad_rows, values, preferred_element_type=jnp.float32)
    dscore = (shares * (grad_probs - row_dot)).astype(jnp.bfloat16)
    grad_query = (
        jnp.einsum("cij,cjd->cid", dscore, key_block, preferred_element_type=jnp.float32) * scaling
    ).astype(jnp.bfloat16)
    key_terms = (
        jnp.einsum("cij,cid->cjd", dscore, query_rows, preferred_element_type=jnp.float32) * scaling
    )
    value_terms = jnp.einsum(
        "cij,cid->cjd", shares_low, grad_rows, preferred_element_type=jnp.float32
    )
    return attended, grad_query, key_terms, value_terms


def attention_kernel(index_ref, flag_ref, q_ref, g_ref, ko_ref, kw_ref, kp_ref, vo_ref, vw_ref, vp_ref, *rest):
    ad_ref, own_ref, win_ref, par_ref = rest[-4:]
    place = pl.program_id(0)
    q = q_ref[0]
    g = g_ref[0]
    keys = (ko_ref[0], kw_ref[0], kp_ref[0])
    values = (vo_ref[0], vw_ref[0], vp_ref[0])
    scaling = 1.0 / math.sqrt(q.shape[-1])
    rows_by_rows = (((1,), (1,)), ((), ()))
    cols_by_cols = (((0,), (0,)), ((), ()))
    scores = [
        lax.dot_general(q, k, rows_by_rows, preferred_element_type=jnp.float32) * scaling
        for k in keys
    ]
    kill = jnp.where(place == 0, flag_ref[0], 0)
    scores[1] = jnp.where(kill > 0, -jnp.inf, scores[1])
    highest = jnp.maximum(
        jnp.maximum(jnp.max(scores[0], axis=1, keepdims=True), jnp.max(scores[1], axis=1, keepdims=True)),
        jnp.max(scores[2], axis=1, keepdims=True),
    )
    weights = [jnp.exp(s - highest) for s in scores]
    total = (
        jnp.sum(weights[0], axis=1, keepdims=True)
        + jnp.sum(weights[1], axis=1, keepdims=True)
        + jnp.sum(weights[2], axis=1, keepdims=True)
    )
    shares = [w / total for w in weights]
    shares_low = [s.astype(jnp.bfloat16) for s in shares]
    attended_wide = jnp.dot(shares_low[0], values[0], preferred_element_type=jnp.float32)
    attended_wide = attended_wide + jnp.dot(shares_low[1], values[1], preferred_element_type=jnp.float32)
    attended_wide = attended_wide + jnp.dot(shares_low[2], values[2], preferred_element_type=jnp.float32)
    attended = attended_wide.astype(jnp.bfloat16)
    ad_ref[0, 0] = attended
    row_dot = jnp.sum(g.astype(jnp.float32) * attended.astype(jnp.float32), axis=1, keepdims=True)
    dq = None
    for part in range(3):
        grad_probs = lax.dot_general(g, values[part], rows_by_rows, preferred_element_type=jnp.float32)
        dscore = (shares[part] * (grad_probs - row_dot)).astype(jnp.bfloat16)
        term = jnp.dot(dscore, keys[part], preferred_element_type=jnp.float32)
        dq = term if dq is None else dq + term
        out_ref = (own_ref.at[0], win_ref.at[0], par_ref.at[0, 0])[part]
        out_ref[0] = (
            lax.dot_general(dscore, q, cols_by_cols, preferred_element_type=jnp.float32) * scaling
        )
        out_ref[1] = lax.dot_general(
            shares_low[part], g, cols_by_cols, preferred_element_type=jnp.float32
        )
    ad_ref[0, 1] = (dq * scaling).astype(jnp.bfloat16)


def fused_terms(parity, q_rows, g_rows, k_all, v_all, k_window, v_window, partner_index, first_masked, partner_buffer=None):
    places, rows, width = q_rows.shape
    row_spec = pl.BlockSpec((1, rows, width), lambda p, idx, flag: (p, 0, 0))
    own_spec = pl.BlockSpec((1, rows, width), lambda p, idx, flag: (2 * p + parity, 0, 0))
    partner_spec = pl.BlockSpec((1, rows, width), lambda p, idx, flag: (idx[p], 0, 0))
    if parity:
        window_spec = pl.BlockSpec((1, rows, width), lambda p, idx, flag: (2 * p, 0, 0))
    else:
        window_spec = row_spec
    pair_spec = pl.BlockSpec((1, 2, rows, width), lambda p, idx, flag: (p, 0, 0, 0))
    target_spec = pl.BlockSpec(
        (1, 1, 2, rows, width), lambda p, idx, flag: (idx[p] % 2, idx[p] // 2, 0, 0, 0)
    )
    in_specs = [row_spec, row_spec, own_spec, window_spec, partner_spec, own_spec, window_spec, partner_spec]
    operands = [partner_index, first_masked, q_rows, g_rows, k_all, k_window, k_all, v_all, v_window, v_all]
    aliases = {}
    if partner_buffer is not None:
        in_specs.append(pl.BlockSpec(memory_space=pl.ANY))
        aliases = {len(operands): 3}
        operands.append(partner_buffer)
    flops = 36 * places * rows * rows * width
    return pl.pallas_call(
        attention_kernel,
        grid_spec=pltpu.PrefetchScalarGridSpec(
            num_scalar_prefetch=2,
            grid=(places,),
            in_specs=in_specs,
            out_specs=[pair_spec, pair_spec, pair_spec, target_spec],
        ),
        out_shape=[jax.ShapeDtypeStruct((places, 2, rows, width), jnp.bfloat16)]
        + [jax.ShapeDtypeStruct((places, 2, rows, width), jnp.float32)] * 2
        + [jax.ShapeDtypeStruct((2, places, 2, rows, width), jnp.float32)],
        input_output_aliases=aliases,
        cost_estimate=pl.CostEstimate(
            flops=flops,
            transcendentals=3 * places * rows * rows,
            bytes_accessed=places * rows * width * 60,
        ),
    )(*operands)


def interleave(even, odd):
    return jnp.stack([even, odd], axis=1).reshape((-1,) + even.shape[1:])


def pick(tree, index):
    return jax.tree.map(lambda x: lax.dynamic_index_in_dim(x, index, axis=0, keepdims=False), tree)


def gather_group(x, within, nseg, group):
    received = [pick(x, within)]
    for shift in range(1, group):
        received.append(lax.ppermute(pick(x, (within + shift) % group), "seq", group_pairs(nseg, group, shift)))

    def place(*pieces):
        out = jnp.zeros((group,) + pieces[0].shape, pieces[0].dtype)
        for shift, piece in enumerate(pieces):
            out = lax.dynamic_update_index_in_dim(out, piece, (within - shift) % group, 0)
        return out

    return jax.tree.map(place, *received)


def scatter_group(y, within, nseg, group):
    returned = [pick(y, within)]
    for shift in range(1, group):
        returned.append(
            lax.ppermute(pick(y, (within - shift) % group), "seq", group_pairs(nseg, group, group - shift))
        )
    return [((within + shift) % group, piece) for shift, piece in enumerate(returned)]


def assemble(even_parts, odd_parts, heads, shape):
    first = even_parts[0][1]
    out = jnp.zeros((heads, 2) + first.shape, first.dtype)
    zero = jnp.zeros((), jnp.int32)
    for column, parts in ((0, even_parts), (1, odd_parts)):
        for head, piece in parts:
            out = lax.dynamic_update_slice(
                out, piece[None, None], (head, jnp.int32(column), zero, zero)
            )
    return out.reshape(shape)


def body(queries, key_rows, value_rows, grad_out, partner_pos):
    heads, row_count, width = queries.shape
    blocks = row_count // BLK
    places = partner_pos.shape[2]
    group = places // blocks
    if heads != group or blocks != 2:
        raise ValueError("layout mismatch")
    nseg = lax.axis_size("seq") // group
    device = lax.axis_index("seq")
    segment = device % nseg
    within = device // nseg

    def split(x):
        return x.reshape(heads, blocks, BLK, width)

    q4, g4, k4, v4 = split(queries), split(grad_out), split(key_rows), split(value_rows)
    kv_local = gather_group(jnp.stack([k4, v4], axis=1), within, nseg, group)
    k_all = kv_local[:, 0].reshape(places, BLK, width)
    v_all = kv_local[:, 1].reshape(places, BLK, width)
    k_all, v_all, qd_odd_send = lax.optimization_barrier(
        (k_all, v_all, jnp.stack([q4[:, 1], g4[:, 1]], axis=1))
    )
    qd_odd = gather_group(qd_odd_send, within, nseg, group)
    q_odd, g_odd = qd_odd[:, 0], qd_odd[:, 1]
    q_odd, g_odd, qd_even_send = lax.optimization_barrier(
        (q_odd, g_odd, jnp.stack([q4[:, 0], g4[:, 0]], axis=1))
    )
    qd_even = gather_group(qd_even_send, within, nseg, group)
    q_even, g_even = qd_even[:, 0], qd_even[:, 1]

    odd_kv = jnp.stack([k_all[1::2], v_all[1::2]], axis=1)
    odd_send = jnp.where(segment == nseg - 1, jnp.roll(odd_kv, 1, axis=0), odd_kv)
    window_kv = lax.ppermute(odd_send, "seq", next_segment_pairs(nseg, group))

    my_partners = lax.dynamic_index_in_dim(
        lax.dynamic_index_in_dim(partner_pos, within, axis=0, keepdims=False),
        segment,
        axis=0,
        keepdims=False,
    )
    no_mask = jnp.zeros((1,), jnp.int32)
    ad_odd, own_odd, win_odd, par_odd = fused_terms(
        1, q_odd, g_odd, k_all, v_all, k_all, v_all, my_partners[1::2], no_mask
    )

    first_masked = (segment == 0).astype(jnp.int32).reshape(1)
    ad_even, own_even, win_even, par_all = fused_terms(
        0, q_even, g_even, k_all, v_all, window_kv[:, 0], window_kv[:, 1], my_partners[0::2], first_masked, par_odd
    )

    ret = win_even
    ret = jnp.where(segment == 0, jnp.roll(ret, -1, axis=0), ret)
    back_pairs = [(b, a) for a, b in next_segment_pairs(nseg, group)]
    window_back = lax.ppermute(ret, "seq", back_pairs)

    partner_even = par_all[0]
    partner_odd = par_all[1]
    grads_even = (own_even + win_odd + partner_even).astype(jnp.bfloat16)
    sent_even = scatter_group(jnp.concatenate([ad_odd, ad_even, grads_even], axis=1), within, nseg, group)
    grads_even, own_odd, partner_odd = lax.optimization_barrier((grads_even, own_odd, partner_odd))
    grads_odd = (own_odd + window_back + partner_odd).astype(jnp.bfloat16)
    sent_last = scatter_group(grads_odd, within, nseg, group)

    shape = (heads, row_count, width)

    def column(parts, index, entry=None):
        if entry is None:
            return [(h, piece[index]) for h, piece in parts]
        return [(h, piece[entry][index]) for h, piece in parts]

    return (
        assemble(column(sent_even, 2), column(sent_even, 0), heads, shape),
        assemble(column(sent_even, 3), column(sent_even, 1), heads, shape),
        assemble(column(sent_even, 4), column(sent_last, 0), heads, shape),
        assemble(column(sent_even, 5), column(sent_last, 1), heads, shape),
    )


def solution(mesh):
    return jax.shard_map(
        body,
        mesh=mesh,
        in_specs=(
            P("head", "seq", None),
            P("head", "seq", None),
            P("head", "seq", None),
            P("head", "seq", None),
            P("head", None, None),
        ),
        out_specs=(
            P("head", "seq", None),
            P("head", "seq", None),
            P("head", "seq", None),
            P("head", "seq", None),
        ),
        check_vma=False,
    )
```

```python
import math

import jax
import jax.numpy as jnp
from jax import lax
from jax.experimental import pallas as pl
from jax.experimental.pallas import tpu as pltpu
from jax.sharding import PartitionSpec as P

BLK = 512


def group_pairs(nseg, group, shift):
    return [
        (seg + nseg * w, seg + nseg * ((w + shift) % group))
        for seg in range(nseg)
        for w in range(group)
    ]


def next_segment_pairs(nseg, group):
    return [
        (seg + nseg * w, (seg + 1) % nseg + nseg * w)
        for seg in range(nseg)
        for w in range(group)
    ]


def block_terms(query_rows, key_block, values, grad_rows, usable):
    scaling = 1.0 / math.sqrt(query_rows.shape[-1])
    scores = (
        jnp.einsum("cid,cjd->cij", query_rows, key_block, preferred_element_type=jnp.float32)
        * scaling
    )
    scores = jnp.where(usable[:, None, :], scores, -jnp.inf)
    highest = jnp.max(scores, axis=2, keepdims=True)
    weights = jnp.exp(scores - highest)
    shares = weights / jnp.sum(weights, axis=2, keepdims=True)
    shares_low = shares.astype(jnp.bfloat16)
    attended = jnp.einsum(
        "cij,cjd->cid", shares_low, values, preferred_element_type=jnp.float32
    ).astype(jnp.bfloat16)
    attended_wide = lax.optimization_barrier(attended).astype(jnp.float32)
    row_dot = jnp.sum(grad_rows.astype(jnp.float32) * attended_wide, axis=2, keepdims=True)
    grad_probs = jnp.einsum("cid,cjd->cij", grad_rows, values, preferred_element_type=jnp.float32)
    dscore = (shares * (grad_probs - row_dot)).astype(jnp.bfloat16)
    grad_query = (
        jnp.einsum("cij,cjd->cid", dscore, key_block, preferred_element_type=jnp.float32) * scaling
    ).astype(jnp.bfloat16)
    key_terms = (
        jnp.einsum("cij,cid->cjd", dscore, query_rows, preferred_element_type=jnp.float32) * scaling
    )
    value_terms = jnp.einsum(
        "cij,cid->cjd", shares_low, grad_rows, preferred_element_type=jnp.float32
    )
    return attended, grad_query, key_terms, value_terms


def attention_kernel(index_ref, flag_ref, q_ref, g_ref, ko_ref, kw_ref, kp_ref, vo_ref, vw_ref, vp_ref, *rest):
    ad_ref, own_ref, win_ref, par_ref = rest[-4:]
    place = pl.program_id(0)
    q = q_ref[0]
    g = g_ref[0]
    keys = (ko_ref[0], kw_ref[0], kp_ref[0])
    values = (vo_ref[0], vw_ref[0], vp_ref[0])
    scaling = 1.0 / math.sqrt(q.shape[-1])
    rows_by_rows = (((1,), (1,)), ((), ()))
    cols_by_cols = (((0,), (0,)), ((), ()))
    scores = [
        lax.dot_general(q, k, rows_by_rows, preferred_element_type=jnp.float32) * scaling
        for k in keys
    ]
    kill = jnp.where(place == 0, flag_ref[0], 0)
    scores[1] = jnp.where(kill > 0, -jnp.inf, scores[1])
    highest = jnp.maximum(
        jnp.maximum(jnp.max(scores[0], axis=1, keepdims=True), jnp.max(scores[1], axis=1, keepdims=True)),
        jnp.max(scores[2], axis=1, keepdims=True),
    )
    weights = [jnp.exp(s - highest) for s in scores]
    total = (
        jnp.sum(weights[0], axis=1, keepdims=True)
        + jnp.sum(weights[1], axis=1, keepdims=True)
        + jnp.sum(weights[2], axis=1, keepdims=True)
    )
    shares = [w / total for w in weights]
    shares_low = [s.astype(jnp.bfloat16) for s in shares]
    attended_wide = jnp.dot(shares_low[0], values[0], preferred_element_type=jnp.float32)
    attended_wide = attended_wide + jnp.dot(shares_low[1], values[1], preferred_element_type=jnp.float32)
    attended_wide = attended_wide + jnp.dot(shares_low[2], values[2], preferred_element_type=jnp.float32)
    attended = attended_wide.astype(jnp.bfloat16)
    ad_ref[0, 0] = attended
    row_dot = jnp.sum(g.astype(jnp.float32) * attended.astype(jnp.float32), axis=1, keepdims=True)
    dq = None
    for part in range(3):
        grad_probs = lax.dot_general(g, values[part], rows_by_rows, preferred_element_type=jnp.float32)
        dscore = (shares[part] * (grad_probs - row_dot)).astype(jnp.bfloat16)
        term = jnp.dot(dscore, keys[part], preferred_element_type=jnp.float32)
        dq = term if dq is None else dq + term
        out_ref = (own_ref.at[0], win_ref.at[0], par_ref.at[0, 0])[part]
        out_ref[0] = (
            lax.dot_general(dscore, q, cols_by_cols, preferred_element_type=jnp.float32) * scaling
        )
        out_ref[1] = lax.dot_general(
            shares_low[part], g, cols_by_cols, preferred_element_type=jnp.float32
        )
    ad_ref[0, 1] = (dq * scaling).astype(jnp.bfloat16)


def fused_terms(parity, q_rows, g_rows, k_all, v_all, k_window, v_window, partner_index, first_masked, partner_buffer=None):
    places, rows, width = q_rows.shape
    row_spec = pl.BlockSpec((1, rows, width), lambda p, idx, flag: (p, 0, 0))
    own_spec = pl.BlockSpec((1, rows, width), lambda p, idx, flag: (2 * p + parity, 0, 0))
    partner_spec = pl.BlockSpec((1, rows, width), lambda p, idx, flag: (idx[p], 0, 0))
    if parity:
        window_spec = pl.BlockSpec((1, rows, width), lambda p, idx, flag: (2 * p, 0, 0))
    else:
        window_spec = row_spec
    pair_spec = pl.BlockSpec((1, 2, rows, width), lambda p, idx, flag: (p, 0, 0, 0))
    target_spec = pl.BlockSpec(
        (1, 1, 2, rows, width), lambda p, idx, flag: (idx[p] % 2, idx[p] // 2, 0, 0, 0)
    )
    in_specs = [row_spec, row_spec, own_spec, window_spec, partner_spec, own_spec, window_spec, partner_spec]
    operands = [partner_index, first_masked, q_rows, g_rows, k_all, k_window, k_all, v_all, v_window, v_all]
    aliases = {}
    if partner_buffer is not None:
        in_specs.append(pl.BlockSpec(memory_space=pl.ANY))
        aliases = {len(operands): 3}
        operands.append(partner_buffer)
    flops = 36 * places * rows * rows * width
    return pl.pallas_call(
        attention_kernel,
        grid_spec=pltpu.PrefetchScalarGridSpec(
            num_scalar_prefetch=2,
            grid=(places,),
            in_specs=in_specs,
            out_specs=[pair_spec, pair_spec, pair_spec, target_spec],
        ),
        out_shape=[jax.ShapeDtypeStruct((places, 2, rows, width), jnp.bfloat16)]
        + [jax.ShapeDtypeStruct((places, 2, rows, width), jnp.float32)] * 2
        + [jax.ShapeDtypeStruct((2, places, 2, rows, width), jnp.float32)],
        input_output_aliases=aliases,
        cost_estimate=pl.CostEstimate(
            flops=flops,
            transcendentals=3 * places * rows * rows,
            bytes_accessed=places * rows * width * 60,
        ),
    )(*operands)


def interleave(even, odd):
    return jnp.stack([even, odd], axis=1).reshape((-1,) + even.shape[1:])


def pick(tree, index):
    return jax.tree.map(lambda x: lax.dynamic_index_in_dim(x, index, axis=0, keepdims=False), tree)


def gather_group(x, within, nseg, group):
    received = [pick(x, within)]
    for shift in range(1, group):
        received.append(lax.ppermute(pick(x, (within + shift) % group), "seq", group_pairs(nseg, group, shift)))

    def place(*pieces):
        out = jnp.zeros((group,) + pieces[0].shape, pieces[0].dtype)
        for shift, piece in enumerate(pieces):
            out = lax.dynamic_update_index_in_dim(out, piece, (within - shift) % group, 0)
        return out

    return jax.tree.map(place, *received)


def scatter_group(y, within, nseg, group):
    returned = [pick(y, within)]
    for shift in range(1, group):
        returned.append(
            lax.ppermute(pick(y, (within - shift) % group), "seq", group_pairs(nseg, group, group - shift))
        )
    return [((within + shift) % group, piece) for shift, piece in enumerate(returned)]


def assemble(even_parts, odd_parts, heads, shape):
    first = even_parts[0][1]
    out = jnp.zeros((heads, 2) + first.shape, first.dtype)
    zero = jnp.zeros((), jnp.int32)
    for column, parts in ((0, even_parts), (1, odd_parts)):
        for head, piece in parts:
            out = lax.dynamic_update_slice(
                out, piece[None, None], (head, jnp.int32(column), zero, zero)
            )
    return out.reshape(shape)


def body(queries, key_rows, value_rows, grad_out, partner_pos):
    heads, row_count, width = queries.shape
    blocks = row_count // BLK
    places = partner_pos.shape[2]
    group = places // blocks
    if heads != group or blocks != 2:
        raise ValueError("layout mismatch")
    nseg = lax.axis_size("seq") // group
    device = lax.axis_index("seq")
    segment = device % nseg
    within = device // nseg

    def split(x):
        return x.reshape(heads, blocks, BLK, width)

    q4, g4, k4, v4 = split(queries), split(grad_out), split(key_rows), split(value_rows)
    first = jnp.concatenate([k4, v4, q4[:, 1:], g4[:, 1:]], axis=1)
    first_local = gather_group(first, within, nseg, group)
    k_all = first_local[:, 0:2].reshape(places, BLK, width)
    v_all = first_local[:, 2:4].reshape(places, BLK, width)
    q_odd, g_odd = first_local[:, 4], first_local[:, 5]
    q_odd, g_odd, qd_even_send = lax.optimization_barrier(
        (q_odd, g_odd, jnp.stack([q4[:, 0], g4[:, 0]], axis=1))
    )
    qd_even = gather_group(qd_even_send, within, nseg, group)
    q_even, g_even = qd_even[:, 0], qd_even[:, 1]

    odd_kv = jnp.stack([k_all[1::2], v_all[1::2]], axis=1)
    odd_send = jnp.where(segment == nseg - 1, jnp.roll(odd_kv, 1, axis=0), odd_kv)
    window_kv = lax.ppermute(odd_send, "seq", next_segment_pairs(nseg, group))

    my_partners = lax.dynamic_index_in_dim(
        lax.dynamic_index_in_dim(partner_pos, within, axis=0, keepdims=False),
        segment,
        axis=0,
        keepdims=False,
    )
    no_mask = jnp.zeros((1,), jnp.int32)
    ad_odd, own_odd, win_odd, par_odd = fused_terms(
        1, q_odd, g_odd, k_all, v_all, k_all, v_all, my_partners[1::2], no_mask
    )
    sent_odd = scatter_group(ad_odd, within, nseg, group)

    first_masked = (segment == 0).astype(jnp.int32).reshape(1)
    ad_even, own_even, win_even, par_all = fused_terms(
        0, q_even, g_even, k_all, v_all, window_kv[:, 0], window_kv[:, 1], my_partners[0::2], first_masked, par_odd
    )

    ret = win_even
    ret = jnp.where(segment == 0, jnp.roll(ret, -1, axis=0), ret)
    back_pairs = [(b, a) for a, b in next_segment_pairs(nseg, group)]
    window_back = lax.ppermute(ret, "seq", back_pairs)

    partner_even = par_all[0]
    partner_odd = par_all[1]
    grads_even = (own_even + win_odd + partner_even).astype(jnp.bfloat16)
    sent_even = scatter_group(jnp.concatenate([ad_even, grads_even], axis=1), within, nseg, group)
    grads_even, own_odd, partner_odd = lax.optimization_barrier((grads_even, own_odd, partner_odd))
    grads_odd = (own_odd + window_back + partner_odd).astype(jnp.bfloat16)
    sent_last = scatter_group(grads_odd, within, nseg, group)

    shape = (heads, row_count, width)

    def column(parts, index, entry=None):
        if entry is None:
            return [(h, piece[index]) for h, piece in parts]
        return [(h, piece[entry][index]) for h, piece in parts]

    return (
        assemble(column(sent_even, 0), column(sent_odd, 0), heads, shape),
        assemble(column(sent_even, 1), column(sent_odd, 1), heads, shape),
        assemble(column(sent_even, 2), column(sent_last, 0), heads, shape),
        assemble(column(sent_even, 3), column(sent_last, 1), heads, shape),
    )


def solution(mesh):
    return jax.shard_map(
        body,
        mesh=mesh,
        in_specs=(
            P("head", "seq", None),
            P("head", "seq", None),
            P("head", "seq", None),
            P("head", "seq", None),
            P("head", None, None),
        ),
        out_specs=(
            P("head", "seq", None),
            P("head", "seq", None),
            P("head", "seq", None),
            P("head", "seq", None),
        ),
        check_vma=False,
    )
```

```python
import math

import jax
import jax.numpy as jnp
from jax import lax
from jax.experimental import pallas as pl
from jax.experimental.pallas import tpu as pltpu
from jax.sharding import PartitionSpec as P

BLK = 512


def group_pairs(nseg, group, shift):
    return [
        (seg + nseg * w, seg + nseg * ((w + shift) % group))
        for seg in range(nseg)
        for w in range(group)
    ]


def next_segment_pairs(nseg, group):
    return [
        (seg + nseg * w, (seg + 1) % nseg + nseg * w)
        for seg in range(nseg)
        for w in range(group)
    ]


def block_terms(query_rows, key_block, values, grad_rows, usable):
    scaling = 1.0 / math.sqrt(query_rows.shape[-1])
    scores = (
        jnp.einsum("cid,cjd->cij", query_rows, key_block, preferred_element_type=jnp.float32)
        * scaling
    )
    scores = jnp.where(usable[:, None, :], scores, -jnp.inf)
    highest = jnp.max(scores, axis=2, keepdims=True)
    weights = jnp.exp(scores - highest)
    shares = weights / jnp.sum(weights, axis=2, keepdims=True)
    shares_low = shares.astype(jnp.bfloat16)
    attended = jnp.einsum(
        "cij,cjd->cid", shares_low, values, preferred_element_type=jnp.float32
    ).astype(jnp.bfloat16)
    attended_wide = lax.optimization_barrier(attended).astype(jnp.float32)
    row_dot = jnp.sum(grad_rows.astype(jnp.float32) * attended_wide, axis=2, keepdims=True)
    grad_probs = jnp.einsum("cid,cjd->cij", grad_rows, values, preferred_element_type=jnp.float32)
    dscore = (shares * (grad_probs - row_dot)).astype(jnp.bfloat16)
    grad_query = (
        jnp.einsum("cij,cjd->cid", dscore, key_block, preferred_element_type=jnp.float32) * scaling
    ).astype(jnp.bfloat16)
    key_terms = (
        jnp.einsum("cij,cid->cjd", dscore, query_rows, preferred_element_type=jnp.float32) * scaling
    )
    value_terms = jnp.einsum(
        "cij,cid->cjd", shares_low, grad_rows, preferred_element_type=jnp.float32
    )
    return attended, grad_query, key_terms, value_terms


def attention_kernel(index_ref, flag_ref, q_ref, g_ref, ko_ref, kw_ref, kp_ref, vo_ref, vw_ref, vp_ref, *rest):
    ad_ref, own_ref, win_ref, par_ref = rest[-4:]
    place = pl.program_id(0)
    q = q_ref[0]
    g = g_ref[0]
    keys = (ko_ref[0], kw_ref[0], kp_ref[0])
    values = (vo_ref[0], vw_ref[0], vp_ref[0])
    scaling = 1.0 / math.sqrt(q.shape[-1])
    rows_by_rows = (((1,), (1,)), ((), ()))
    cols_by_cols = (((0,), (0,)), ((), ()))
    scores = [
        lax.dot_general(q, k, rows_by_rows, preferred_element_type=jnp.float32) * scaling
        for k in keys
    ]
    kill = jnp.where(place == 0, flag_ref[0], 0)
    scores[1] = jnp.where(kill > 0, -jnp.inf, scores[1])
    highest = jnp.maximum(
        jnp.maximum(jnp.max(scores[0], axis=1, keepdims=True), jnp.max(scores[1], axis=1, keepdims=True)),
        jnp.max(scores[2], axis=1, keepdims=True),
    )
    weights = [jnp.exp(s - highest) for s in scores]
    total = (
        jnp.sum(weights[0], axis=1, keepdims=True)
        + jnp.sum(weights[1], axis=1, keepdims=True)
        + jnp.sum(weights[2], axis=1, keepdims=True)
    )
    shares = [w / total for w in weights]
    shares_low = [s.astype(jnp.bfloat16) for s in shares]
    attended_wide = jnp.dot(shares_low[0], values[0], preferred_element_type=jnp.float32)
    attended_wide = attended_wide + jnp.dot(shares_low[1], values[1], preferred_element_type=jnp.float32)
    attended_wide = attended_wide + jnp.dot(shares_low[2], values[2], preferred_element_type=jnp.float32)
    attended = attended_wide.astype(jnp.bfloat16)
    ad_ref[0, 0] = attended
    row_dot = jnp.sum(g.astype(jnp.float32) * attended.astype(jnp.float32), axis=1, keepdims=True)
    dq = None
    for part in range(3):
        grad_probs = lax.dot_general(g, values[part], rows_by_rows, preferred_element_type=jnp.float32)
        dscore = (shares[part] * (grad_probs - row_dot)).astype(jnp.bfloat16)
        term = jnp.dot(dscore, keys[part], preferred_element_type=jnp.float32)
        dq = term if dq is None else dq + term
        out_ref = (own_ref.at[0], win_ref.at[0], par_ref.at[0, 0])[part]
        out_ref[0] = (
            lax.dot_general(dscore, q, cols_by_cols, preferred_element_type=jnp.float32) * scaling
        )
        out_ref[1] = lax.dot_general(
            shares_low[part], g, cols_by_cols, preferred_element_type=jnp.float32
        )
    ad_ref[0, 1] = (dq * scaling).astype(jnp.bfloat16)


def fused_terms(parity, q_rows, g_rows, k_all, v_all, k_window, v_window, partner_index, first_masked, partner_buffer=None):
    places, rows, width = q_rows.shape
    row_spec = pl.BlockSpec((1, rows, width), lambda p, idx, flag: (p, 0, 0))
    own_spec = pl.BlockSpec((1, rows, width), lambda p, idx, flag: (2 * p + parity, 0, 0))
    partner_spec = pl.BlockSpec((1, rows, width), lambda p, idx, flag: (idx[p], 0, 0))
    if parity:
        window_spec = pl.BlockSpec((1, rows, width), lambda p, idx, flag: (2 * p, 0, 0))
    else:
        window_spec = row_spec
    pair_spec = pl.BlockSpec((1, 2, rows, width), lambda p, idx, flag: (p, 0, 0, 0))
    target_spec = pl.BlockSpec(
        (1, 1, 2, rows, width), lambda p, idx, flag: (idx[p] % 2, idx[p] // 2, 0, 0, 0)
    )
    in_specs = [row_spec, row_spec, own_spec, window_spec, partner_spec, own_spec, window_spec, partner_spec]
    operands = [partner_index, first_masked, q_rows, g_rows, k_all, k_window, k_all, v_all, v_window, v_all]
    aliases = {}
    if partner_buffer is not None:
        in_specs.append(pl.BlockSpec(memory_space=pl.ANY))
        aliases = {len(operands): 3}
        operands.append(partner_buffer)
    flops = 36 * places * rows * rows * width
    return pl.pallas_call(
        attention_kernel,
        grid_spec=pltpu.PrefetchScalarGridSpec(
            num_scalar_prefetch=2,
            grid=(places,),
            in_specs=in_specs,
            out_specs=[pair_spec, pair_spec, pair_spec, target_spec],
        ),
        out_shape=[jax.ShapeDtypeStruct((places, 2, rows, width), jnp.bfloat16)]
        + [jax.ShapeDtypeStruct((places, 2, rows, width), jnp.float32)] * 2
        + [jax.ShapeDtypeStruct((2, places, 2, rows, width), jnp.float32)],
        input_output_aliases=aliases,
        cost_estimate=pl.CostEstimate(
            flops=flops,
            transcendentals=3 * places * rows * rows,
            bytes_accessed=places * rows * width * 60,
        ),
    )(*operands)


def interleave(even, odd):
    return jnp.stack([even, odd], axis=1).reshape((-1,) + even.shape[1:])


def pick(tree, index):
    return jax.tree.map(lambda x: lax.dynamic_index_in_dim(x, index, axis=0, keepdims=False), tree)


def gather_group(x, within, nseg, group):
    received = [pick(x, within)]
    for shift in range(1, group):
        received.append(lax.ppermute(pick(x, (within + shift) % group), "seq", group_pairs(nseg, group, shift)))

    def place(*pieces):
        out = jnp.zeros((group,) + pieces[0].shape, pieces[0].dtype)
        for shift, piece in enumerate(pieces):
            out = lax.dynamic_update_index_in_dim(out, piece, (within - shift) % group, 0)
        return out

    return jax.tree.map(place, *received)


def scatter_group(y, within, nseg, group):
    returned = [pick(y, within)]
    for shift in range(1, group):
        returned.append(
            lax.ppermute(pick(y, (within - shift) % group), "seq", group_pairs(nseg, group, group - shift))
        )
    return [((within + shift) % group, piece) for shift, piece in enumerate(returned)]


def assemble(even_parts, odd_parts, heads, shape):
    first = even_parts[0][1]
    out = jnp.zeros((heads, 2) + first.shape, first.dtype)
    zero = jnp.zeros((), jnp.int32)
    for column, parts in ((0, even_parts), (1, odd_parts)):
        for head, piece in parts:
            out = lax.dynamic_update_slice(
                out, piece[None, None], (head, jnp.int32(column), zero, zero)
            )
    return out.reshape(shape)


def body(queries, key_rows, value_rows, grad_out, partner_pos):
    heads, row_count, width = queries.shape
    blocks = row_count // BLK
    places = partner_pos.shape[2]
    group = places // blocks
    if heads != group or blocks != 2:
        raise ValueError("layout mismatch")
    nseg = lax.axis_size("seq") // group
    device = lax.axis_index("seq")
    segment = device % nseg
    within = device // nseg

    def split(x):
        return x.reshape(heads, blocks, BLK, width)

    q4, g4, k4, v4 = split(queries), split(grad_out), split(key_rows), split(value_rows)
    first = jnp.concatenate([k4, v4, q4[:, 1:], g4[:, 1:]], axis=1)
    first_local = gather_group(first, within, nseg, group)
    k_all = first_local[:, 0:2].reshape(places, BLK, width)
    v_all = first_local[:, 2:4].reshape(places, BLK, width)
    q_odd, g_odd = first_local[:, 4], first_local[:, 5]
    q_odd, g_odd, qd_even_send = lax.optimization_barrier(
        (q_odd, g_odd, jnp.stack([q4[:, 0], g4[:, 0]], axis=1))
    )
    qd_even = gather_group(qd_even_send, within, nseg, group)
    q_even, g_even = qd_even[:, 0], qd_even[:, 1]

    odd_kv = jnp.stack([k_all[1::2], v_all[1::2]], axis=1)
    odd_send = jnp.where(segment == nseg - 1, jnp.roll(odd_kv, 1, axis=0), odd_kv)
    window_kv = lax.ppermute(odd_send, "seq", next_segment_pairs(nseg, group))

    my_partners = lax.dynamic_index_in_dim(
        lax.dynamic_index_in_dim(partner_pos, within, axis=0, keepdims=False),
        segment,
        axis=0,
        keepdims=False,
    )
    no_mask = jnp.zeros((1,), jnp.int32)
    ad_odd, own_odd, win_odd, par_odd = fused_terms(
        1, q_odd, g_odd, k_all, v_all, k_all, v_all, my_partners[1::2], no_mask
    )
    sent_odd = scatter_group(ad_odd, within, nseg, group)

    first_masked = (segment == 0).astype(jnp.int32).reshape(1)
    ad_even, own_even, win_even, par_all = fused_terms(
        0, q_even, g_even, k_all, v_all, window_kv[:, 0], window_kv[:, 1], my_partners[0::2], first_masked, par_odd
    )

    ret = win_even
    ret = jnp.where(segment == 0, jnp.roll(ret, -1, axis=0), ret)
    back_pairs = [(b, a) for a, b in next_segment_pairs(nseg, group)]
    window_back = lax.ppermute(ret.astype(jnp.bfloat16), "seq", back_pairs)
    sent_even = scatter_group(ad_even, within, nseg, group)

    partner_even = par_all[0]
    partner_odd = par_all[1]
    grads_even = (own_even + win_odd + partner_even).astype(jnp.bfloat16)
    grads_odd = (own_odd + window_back.astype(jnp.float32) + partner_odd).astype(jnp.bfloat16)
    sent_last = scatter_group(jnp.concatenate([grads_even, grads_odd], axis=1), within, nseg, group)

    shape = (heads, row_count, width)

    def column(parts, index, entry=None):
        if entry is None:
            return [(h, piece[index]) for h, piece in parts]
        return [(h, piece[entry][index]) for h, piece in parts]

    return (
        assemble(column(sent_even, 0), column(sent_odd, 0), heads, shape),
        assemble(column(sent_even, 1), column(sent_odd, 1), heads, shape),
        assemble(column(sent_last, 0), column(sent_last, 2), heads, shape),
        assemble(column(sent_last, 1), column(sent_last, 3), heads, shape),
    )


def solution(mesh):
    return jax.shard_map(
        body,
        mesh=mesh,
        in_specs=(
            P("head", "seq", None),
            P("head", "seq", None),
            P("head", "seq", None),
            P("head", "seq", None),
            P("head", None, None),
        ),
        out_specs=(
            P("head", "seq", None),
            P("head", "seq", None),
            P("head", "seq", None),
            P("head", "seq", None),
        ),
        check_vma=False,
    )
```

```python
import math

import jax
import jax.numpy as jnp
from jax import lax
from jax.experimental import pallas as pl
from jax.experimental.pallas import tpu as pltpu
from jax.sharding import PartitionSpec as P

BLK = 512


def group_pairs(nseg, group, shift):
    return [
        (seg + nseg * w, seg + nseg * ((w + shift) % group))
        for seg in range(nseg)
        for w in range(group)
    ]


def next_segment_pairs(nseg, group):
    return [
        (seg + nseg * w, (seg + 1) % nseg + nseg * w)
        for seg in range(nseg)
        for w in range(group)
    ]


def block_terms(query_rows, key_block, values, grad_rows, usable):
    scaling = 1.0 / math.sqrt(query_rows.shape[-1])
    scores = (
        jnp.einsum("cid,cjd->cij", query_rows, key_block, preferred_element_type=jnp.float32)
        * scaling
    )
    scores = jnp.where(usable[:, None, :], scores, -jnp.inf)
    highest = jnp.max(scores, axis=2, keepdims=True)
    weights = jnp.exp(scores - highest)
    shares = weights / jnp.sum(weights, axis=2, keepdims=True)
    shares_low = shares.astype(jnp.bfloat16)
    attended = jnp.einsum(
        "cij,cjd->cid", shares_low, values, preferred_element_type=jnp.float32
    ).astype(jnp.bfloat16)
    attended_wide = lax.optimization_barrier(attended).astype(jnp.float32)
    row_dot = jnp.sum(grad_rows.astype(jnp.float32) * attended_wide, axis=2, keepdims=True)
    grad_probs = jnp.einsum("cid,cjd->cij", grad_rows, values, preferred_element_type=jnp.float32)
    dscore = (shares * (grad_probs - row_dot)).astype(jnp.bfloat16)
    grad_query = (
        jnp.einsum("cij,cjd->cid", dscore, key_block, preferred_element_type=jnp.float32) * scaling
    ).astype(jnp.bfloat16)
    key_terms = (
        jnp.einsum("cij,cid->cjd", dscore, query_rows, preferred_element_type=jnp.float32) * scaling
    )
    value_terms = jnp.einsum(
        "cij,cid->cjd", shares_low, grad_rows, preferred_element_type=jnp.float32
    )
    return attended, grad_query, key_terms, value_terms


def attention_kernel(index_ref, flag_ref, q_ref, g_ref, ko_ref, kw_ref, kp_ref, vo_ref, vw_ref, vp_ref, *rest):
    ad_ref, own_ref, win_ref, par_ref = rest[-4:]
    place = pl.program_id(0)
    q = q_ref[0]
    g = g_ref[0]
    keys = (ko_ref[0], kw_ref[0], kp_ref[0])
    values = (vo_ref[0], vw_ref[0], vp_ref[0])
    scaling = 1.0 / math.sqrt(q.shape[-1])
    rows_by_rows = (((1,), (1,)), ((), ()))
    cols_by_cols = (((0,), (0,)), ((), ()))
    scores = [
        lax.dot_general(q, k, rows_by_rows, preferred_element_type=jnp.float32) * scaling
        for k in keys
    ]
    kill = jnp.where(place == 0, flag_ref[0], 0)
    scores[1] = jnp.where(kill > 0, -jnp.inf, scores[1])
    highest = jnp.maximum(
        jnp.maximum(jnp.max(scores[0], axis=1, keepdims=True), jnp.max(scores[1], axis=1, keepdims=True)),
        jnp.max(scores[2], axis=1, keepdims=True),
    )
    weights = [jnp.exp(s - highest) for s in scores]
    total = (
        jnp.sum(weights[0], axis=1, keepdims=True)
        + jnp.sum(weights[1], axis=1, keepdims=True)
        + jnp.sum(weights[2], axis=1, keepdims=True)
    )
    shares = [w / total for w in weights]
    shares_low = [s.astype(jnp.bfloat16) for s in shares]
    attended_wide = jnp.dot(shares_low[0], values[0], preferred_element_type=jnp.float32)
    attended_wide = attended_wide + jnp.dot(shares_low[1], values[1], preferred_element_type=jnp.float32)
    attended_wide = attended_wide + jnp.dot(shares_low[2], values[2], preferred_element_type=jnp.float32)
    attended = attended_wide.astype(jnp.bfloat16)
    ad_ref[0, 0] = attended
    row_dot = jnp.sum(g.astype(jnp.float32) * attended.astype(jnp.float32), axis=1, keepdims=True)
    dq = None
    for part in range(3):
        grad_probs = lax.dot_general(g, values[part], rows_by_rows, preferred_element_type=jnp.float32)
        dscore = (shares[part] * (grad_probs - row_dot)).astype(jnp.bfloat16)
        term = jnp.dot(dscore, keys[part], preferred_element_type=jnp.float32)
        dq = term if dq is None else dq + term
        out_ref = (own_ref.at[0], win_ref.at[0], par_ref.at[0, 0])[part]
        out_ref[0] = (
            lax.dot_general(dscore, q, cols_by_cols, preferred_element_type=jnp.float32) * scaling
        )
        out_ref[1] = lax.dot_general(
            shares_low[part], g, cols_by_cols, preferred_element_type=jnp.float32
        )
    ad_ref[0, 1] = (dq * scaling).astype(jnp.bfloat16)


def fused_terms(parity, q_rows, g_rows, k_all, v_all, k_window, v_window, partner_index, first_masked, partner_buffer=None):
    places, rows, width = q_rows.shape
    row_spec = pl.BlockSpec((1, rows, width), lambda p, idx, flag: (p, 0, 0))
    own_spec = pl.BlockSpec((1, rows, width), lambda p, idx, flag: (2 * p + parity, 0, 0))
    partner_spec = pl.BlockSpec((1, rows, width), lambda p, idx, flag: (idx[p], 0, 0))
    if parity:
        window_spec = pl.BlockSpec((1, rows, width), lambda p, idx, flag: (2 * p, 0, 0))
    else:
        window_spec = row_spec
    pair_spec = pl.BlockSpec((1, 2, rows, width), lambda p, idx, flag: (p, 0, 0, 0))
    target_spec = pl.BlockSpec(
        (1, 1, 2, rows, width), lambda p, idx, flag: (idx[p] % 2, idx[p] // 2, 0, 0, 0)
    )
    in_specs = [row_spec, row_spec, own_spec, window_spec, partner_spec, own_spec, window_spec, partner_spec]
    operands = [partner_index, first_masked, q_rows, g_rows, k_all, k_window, k_all, v_all, v_window, v_all]
    aliases = {}
    if partner_buffer is not None:
        in_specs.append(pl.BlockSpec(memory_space=pl.ANY))
        aliases = {len(operands): 3}
        operands.append(partner_buffer)
    flops = 36 * places * rows * rows * width
    return pl.pallas_call(
        attention_kernel,
        grid_spec=pltpu.PrefetchScalarGridSpec(
            num_scalar_prefetch=2,
            grid=(places,),
            in_specs=in_specs,
            out_specs=[pair_spec, pair_spec, pair_spec, target_spec],
        ),
        out_shape=[jax.ShapeDtypeStruct((places, 2, rows, width), jnp.bfloat16)]
        + [jax.ShapeDtypeStruct((places, 2, rows, width), jnp.float32)] * 2
        + [jax.ShapeDtypeStruct((2, places, 2, rows, width), jnp.float32)],
        input_output_aliases=aliases,
        cost_estimate=pl.CostEstimate(
            flops=flops,
            transcendentals=3 * places * rows * rows,
            bytes_accessed=places * rows * width * 60,
        ),
    )(*operands)


def interleave(even, odd):
    return jnp.stack([even, odd], axis=1).reshape((-1,) + even.shape[1:])


def pick(tree, index):
    return jax.tree.map(lambda x: lax.dynamic_index_in_dim(x, index, axis=0, keepdims=False), tree)


def gather_group(x, within, nseg, group):
    received = [pick(x, within)]
    for shift in range(1, group):
        received.append(lax.ppermute(pick(x, (within + shift) % group), "seq", group_pairs(nseg, group, shift)))

    def place(*pieces):
        out = jnp.zeros((group,) + pieces[0].shape, pieces[0].dtype)
        for shift, piece in enumerate(pieces):
            out = lax.dynamic_update_index_in_dim(out, piece, (within - shift) % group, 0)
        return out

    return jax.tree.map(place, *received)


def scatter_group(y, within, nseg, group):
    returned = [pick(y, within)]
    for shift in range(1, group):
        returned.append(
            lax.ppermute(pick(y, (within - shift) % group), "seq", group_pairs(nseg, group, group - shift))
        )
    return [((within + shift) % group, piece) for shift, piece in enumerate(returned)]


def assemble(even_parts, odd_parts, heads, shape):
    first = even_parts[0][1]
    out = jnp.zeros((heads, 2) + first.shape, first.dtype)
    zero = jnp.zeros((), jnp.int32)
    for column, parts in ((0, even_parts), (1, odd_parts)):
        for head, piece in parts:
            out = lax.dynamic_update_slice(
                out, piece[None, None], (head, jnp.int32(column), zero, zero)
            )
    return out.reshape(shape)


def body(queries, key_rows, value_rows, grad_out, partner_pos):
    heads, row_count, width = queries.shape
    blocks = row_count // BLK
    places = partner_pos.shape[2]
    group = places // blocks
    if heads != group or blocks != 2:
        raise ValueError("layout mismatch")
    nseg = lax.axis_size("seq") // group
    device = lax.axis_index("seq")
    segment = device % nseg
    within = device // nseg

    def split(x):
        return x.reshape(heads, blocks, BLK, width)

    q4, g4, k4, v4 = split(queries), split(grad_out), split(key_rows), split(value_rows)
    first = jnp.concatenate([k4, v4, q4[:, 1:], g4[:, 1:]], axis=1)
    first_local = gather_group(first, within, nseg, group)
    k_all = first_local[:, 0:2].reshape(places, BLK, width)
    v_all = first_local[:, 2:4].reshape(places, BLK, width)
    q_odd, g_odd = first_local[:, 4], first_local[:, 5]
    q_odd, g_odd, qd_even_send = lax.optimization_barrier(
        (q_odd, g_odd, jnp.stack([q4[:, 0], g4[:, 0]], axis=1))
    )
    qd_even = gather_group(qd_even_send, within, nseg, group)
    q_even, g_even = qd_even[:, 0], qd_even[:, 1]

    odd_kv = jnp.stack([k_all[1::2], v_all[1::2]], axis=1)
    odd_send = jnp.where(segment == nseg - 1, jnp.roll(odd_kv, 1, axis=0), odd_kv)
    window_kv = lax.ppermute(odd_send, "seq", next_segment_pairs(nseg, group))

    my_partners = lax.dynamic_index_in_dim(
        lax.dynamic_index_in_dim(partner_pos, within, axis=0, keepdims=False),
        segment,
        axis=0,
        keepdims=False,
    )
    no_mask = jnp.zeros((1,), jnp.int32)
    ad_odd, own_odd, win_odd, par_odd = fused_terms(
        1, q_odd, g_odd, k_all, v_all, k_all, v_all, my_partners[1::2], no_mask
    )
    sent_odd = scatter_group(ad_odd, within, nseg, group)

    first_masked = (segment == 0).astype(jnp.int32).reshape(1)
    ad_even, own_even, win_even, par_all = fused_terms(
        0, q_even, g_even, k_all, v_all, window_kv[:, 0], window_kv[:, 1], my_partners[0::2], first_masked, par_odd
    )

    ret = win_even
    ret = jnp.where(segment == 0, jnp.roll(ret, -1, axis=0), ret)
    back_pairs = [(b, a) for a, b in next_segment_pairs(nseg, group)]
    window_back = lax.ppermute(ret.astype(jnp.bfloat16), "seq", back_pairs)
    sent_even = scatter_group(ad_even, within, nseg, group)

    partner_even = par_all[0]
    partner_odd = par_all[1]
    grads_even = (own_even + win_odd + partner_even).astype(jnp.bfloat16)
    sent_grads = scatter_group(grads_even, within, nseg, group)
    grads_even, own_odd, partner_odd = lax.optimization_barrier((grads_even, own_odd, partner_odd))
    grads_odd = (own_odd + window_back.astype(jnp.float32) + partner_odd).astype(jnp.bfloat16)
    sent_last = scatter_group(grads_odd, within, nseg, group)

    shape = (heads, row_count, width)

    def column(parts, index, entry=None):
        if entry is None:
            return [(h, piece[index]) for h, piece in parts]
        return [(h, piece[entry][index]) for h, piece in parts]

    return (
        assemble(column(sent_even, 0), column(sent_odd, 0), heads, shape),
        assemble(column(sent_even, 1), column(sent_odd, 1), heads, shape),
        assemble(column(sent_grads, 0), column(sent_last, 0), heads, shape),
        assemble(column(sent_grads, 1), column(sent_last, 1), heads, shape),
    )


def solution(mesh):
    return jax.shard_map(
        body,
        mesh=mesh,
        in_specs=(
            P("head", "seq", None),
            P("head", "seq", None),
            P("head", "seq", None),
            P("head", "seq", None),
            P("head", None, None),
        ),
        out_specs=(
            P("head", "seq", None),
            P("head", "seq", None),
            P("head", "seq", None),
            P("head", "seq", None),
        ),
        check_vma=False,
    )
```
